256 devices in a mesh: rad: 16 (over z, core), azi: 16 (over x, y).
Axes of the slice: x: 4, y: 4, z: 8, core: 2. Of those that a mesh axis runs over, the one named last changes fastest.
Arguments:
- jacobian: bfloat16 [64, 128, 5, 128, 128], P('rad', 'azi')
- new_block: bfloat16 [64, 128, 32, 128], P('rad', 'azi')
- kept: float32 [64, 128, 192, 128], P('rad', 'azi')
- columns: int32 [64, 128, 5], P('rad', 'azi'), may hold values from 0 to 8, as said below
Outputs:
- basis: float32 [64, 128, 32, 128], P('rad', 'azi')
- coefficients: float32 [192, 32], replicated
- factor: float32 [32, 32], replicated
The draws below stay inside these ranges and needn't reach their ends.
Inputs may be any that keep to these rules, and one draw needn't show every extreme that they name: `columns`: slot 0 of every element is 4, the element itself; slots 1 to 4 name four different codes other than 4.
All inputs are finite; a program needn't handle non-finite values.
Results may differ from the reference program's by a relative error of at most 0.0003.
Values may be sent and summed in bfloat16 or wider, within the bound.
No kernel may reach another device: no remote copies, remote signals or barrier semaphores. Data moves between devices by JAX's collectives and lax.ppermute only.
A program may use at most 64 MiB of HBM per device.

```python
import math
import jax
import jax.numpy as jnp
from jax import lax

BLK = 128
NEW = 32
KEEP = 192
NER = 64
NEA = 128
TOTAL = 1048576


def row_profile(key):
    second_key = jax.random.fold_in(jax.random.fold_in(key, 11), 1)
    spread = 10.0
    row_scale = jnp.exp(jax.random.uniform(second_key, (NER, NEA, 1, BLK, 1), jnp.float32) * math.log(spread))
    radial = jnp.arange(NER, dtype=jnp.float32) / max(NER - 1, 1)
    radial = jnp.sqrt(1.0 + 2.0 * radial)[:, None, None, None, None]
    mean_square = 2.0 * (spread * spread - 1.0) / (2.0 * math.log(spread))
    return (row_scale * radial, mean_square)


def fresh_vectors(key):
    vector_key = jax.random.fold_in(key, 31)
    shape = (NER, NEA, NEW, BLK)
    values = jnp.clip(jax.random.normal(vector_key, shape, jnp.float32), -6.0, 6.0)
    return values


def draw_columns(key, part):
    scores = jax.random.randint(jax.random.fold_in(key, 3), (NER, NEA, 8), 0, 1 << 20)
    scores = scores * 8 + jnp.arange(8, dtype=jnp.int32)
    order = jax.lax.top_k(scores, 4)[1].astype(jnp.int32)
    codes = order + (order >= 4).astype(jnp.int32)
    itself = jnp.full((NER, NEA, 1), 4, jnp.int32)
    return jnp.concatenate([itself, codes], axis=2)


def draw_new_block(key, part):
    return fresh_vectors(key).astype(jnp.bfloat16)


def draw_jacobian(key, part):
    first_key = jax.random.fold_in(jax.random.fold_in(key, 11), 0)
    shape = (NER, NEA, 5, BLK, BLK)
    base = jax.random.normal(first_key, shape, jnp.float32)
    profile, mean_square = row_profile(key)
    self_slot = (jnp.arange(5) == 0).astype(jnp.float32)[:, None, None]
    identity = jnp.eye(BLK, dtype=jnp.float32)[None, :, :]
    values = (base / math.sqrt(5.0 * BLK) + 1.5 * self_slot * identity) * profile
    return values.astype(jnp.bfloat16)


def draw_kept(key, part):
    first_key, second_key = jax.random.split(jax.random.fold_in(key, 23))
    base = jax.random.normal(first_key, (NER, NEA, KEEP, BLK), jnp.float32)
    shared = math.sqrt(0.4 / KEEP)
    common = jax.random.normal(second_key, (NER, NEA, 1, BLK), jnp.float32)
    profile, mean_square = row_profile(key)
    lifted = fresh_vectors(key) * profile[:, :, :, :, 0] / math.sqrt(mean_square)
    owner = jax.random.permutation(jax.random.fold_in(key, 41), KEEP).astype(jnp.int32)
    holder = (owner < NEW).astype(jnp.float32)
    chosen = jnp.take(lifted, jnp.minimum(owner, NEW - 1), axis=2) * holder[None, None, :, None]
    weight = 2.0
    norm_square = 1.0 + shared * shared + weight * weight * holder
    scaled = (base + shared * common + weight * chosen) / jnp.sqrt(norm_square * TOTAL)[None, None, :, None]
    return scaled


def setup_inputs(seed: int = 0) -> dict:
    seeds = jax.random.split(jax.random.key(seed), 5)
    jacobian = draw_jacobian(jax.random.fold_in(seeds[4], 71), 0)
    new_block = draw_new_block(jax.random.fold_in(seeds[4], 71), 0)
    kept = draw_kept(jax.random.fold_in(seeds[4], 71), 0)
    columns = draw_columns(jax.random.fold_in(seeds[4], 71), 0)
    return dict(jacobian=jacobian, new_block=new_block, kept=kept, columns=columns)


def reference(jacobian, new_block, kept, columns):
    high = lax.Precision.HIGHEST
    padded = jnp.concatenate([new_block[:, -1:], new_block, new_block[:, :1]], axis=1)
    zero_row = jnp.zeros_like(padded[:1])
    padded = jnp.concatenate([zero_row, padded, zero_row], axis=0)
    stride = jnp.arange(NEA, dtype=jnp.int32)

    def one_row(r):
        triple = lax.dynamic_slice_in_dim(padded, r, 3, 0)
        nine = jnp.stack([triple[i, j:j + NEA] for i in range(3) for j in range(3)], axis=0)
        codes = lax.dynamic_index_in_dim(columns, r, 0, keepdims=False).astype(jnp.int32)
        picked = nine[codes, stride[:, None]]
        block = lax.dynamic_index_in_dim(jacobian, r, 0, keepdims=False)
        return jnp.einsum('akij,akvj->avi', block.astype(jnp.float32), picked.astype(jnp.float32), precision=high)
    image = lax.map(one_row, jnp.arange(NER, dtype=jnp.int32))
    first = jnp.einsum('rapi,ravi->pv', kept, image, precision=high)
    once = image - jnp.einsum('rapi,pv->ravi', kept, first, precision=high)
    second = jnp.einsum('rapi,ravi->pv', kept, once, precision=high)
    twice = once - jnp.einsum('rapi,pv->ravi', kept, second, precision=high)
    gram = jnp.einsum('ravi,rawi->vw', twice, twice, precision=high) / TOTAL
    lower = jnp.linalg.cholesky(gram)
    flat = jnp.moveaxis(twice, 2, 0).reshape(NEW, NER * NEA * BLK)
    solved = lax.linalg.triangular_solve(lower, flat, left_side=True, lower=True)
    basis = jnp.moveaxis(solved.reshape(NEW, NER, NEA, BLK), 0, 2)
    return (basis, first + second, lower.T)
```

```python
import jax
import jax.numpy as jnp
from jax import lax
from jax.sharding import PartitionSpec as P

BLK = 128
NEW = 32
KEEP = 192


def all_sum(x):
    for axis in ("rad", "azi"):
        count = lax.axis_size(axis)
        step = 1
        while step < count:
            x = x + lax.ppermute(x, axis, [(i, i ^ step) for i in range(count)])
            step *= 2
    return x


def with_halo(cells):
    n_r = lax.axis_size("rad")
    n_a = lax.axis_size("azi")
    rows_r, rows_a = cells.shape[0], cells.shape[1]

    def shift_azi(x, d):
        return lax.ppermute(x, "azi", [(i, (i + d) % n_a) for i in range(n_a)])

    def shift_rad(x, d):
        pairs = [(i, i + d) for i in range(n_r) if 0 <= i + d < n_r]
        return lax.ppermute(x, "rad", pairs)

    def shift_both(x, dr, da):
        pairs = []
        for r in range(n_r):
            if 0 <= r + dr < n_r:
                for a in range(n_a):
                    pairs.append((r * n_a + a, (r + dr) * n_a + (a + da) % n_a))
        return lax.ppermute(x, ("rad", "azi"), pairs)

    first_a, last_a = cells[:, :1], cells[:, rows_a - 1 :]
    first_r, last_r = cells[:1], cells[rows_r - 1 :]
    west = shift_azi(last_a, 1)
    east = shift_azi(first_a, -1)
    north = shift_rad(last_r, 1)
    south = shift_rad(first_r, -1)
    nw = shift_both(cells[rows_r - 1 :, rows_a - 1 :], 1, 1)
    ne = shift_both(cells[rows_r - 1 :, :1], 1, -1)
    sw = shift_both(cells[:1, rows_a - 1 :], -1, 1)
    se = shift_both(cells[:1, :1], -1, -1)
    top = jnp.concatenate([nw, north, ne], axis=1)
    middle = jnp.concatenate([west, cells, east], axis=1)
    bottom = jnp.concatenate([sw, south, se], axis=1)
    return jnp.concatenate([top, middle, bottom], axis=0)


def on_device(jacobian, new_block, kept, columns):
    high = lax.Precision.HIGHEST
    rows_r = new_block.shape[0]
    rows_a = new_block.shape[1]
    elements = rows_r * rows_a
    total_rows = elements * BLK * lax.axis_size("rad") * lax.axis_size("azi")
    kept_flat = kept.reshape(elements, KEEP, BLK)

    kept_gram = all_sum(
        jnp.einsum("epi,eqi->pq", kept_flat, kept_flat, precision=high,
                   preferred_element_type=jnp.float32)
    )

    padded = with_halo(new_block)
    shifted = [padded[c // 3 : c // 3 + rows_r, c % 3 : c % 3 + rows_a] for c in range(9)]
    slots = []
    for k in range(5):
        code = columns[:, :, k][:, :, None, None]
        pick = shifted[0]
        for c in range(1, 9):
            pick = jnp.where(code == c, shifted[c], pick)
        slots.append(pick)
    picked = jnp.stack(slots, axis=2)
    image = jnp.einsum("rakij,rakvj->ravi", jacobian, picked, preferred_element_type=jnp.float32)
    image = image.reshape(elements, NEW, BLK)

    first = all_sum(
        jnp.einsum("epi,evi->pv", kept_flat, image, precision=high,
                   preferred_element_type=jnp.float32)
    )
    second = first - jnp.dot(kept_gram, first, precision=high, preferred_element_type=jnp.float32)
    coefficients = first + second
    twice = image - jnp.einsum(
        "epi,pv->evi", kept_flat, coefficients, precision=high, preferred_element_type=jnp.float32
    )
    gram = all_sum(
        jnp.einsum("evi,ewi->vw", twice, twice, precision=high, preferred_element_type=jnp.float32)
    ) / total_rows
    lower = jnp.linalg.cholesky(gram)
    flat = jnp.moveaxis(twice, 1, 0).reshape(NEW, elements * BLK)
    solved = lax.linalg.triangular_solve(lower, flat, left_side=True, lower=True)
    basis = jnp.moveaxis(solved.reshape(NEW, elements, BLK), 0, 1).reshape(rows_r, rows_a, NEW, BLK)
    return (basis, coefficients, lower.T)


def solution(mesh):
    return jax.shard_map(
        on_device,
        mesh=mesh,
        in_specs=(
            P("rad", "azi", None, None, None),
            P("rad", "azi", None, None),
            P("rad", "azi", None, None),
            P("rad", "azi", None),
        ),
        out_specs=(P("rad", "azi", None, None), P(), P()),
        check_vma=False,
    )
```

```python
import jax
import jax.numpy as jnp
from jax import lax
from jax.sharding import PartitionSpec as P

BLK = 128
NEW = 32
KEEP = 192


def all_sum(x):
    for axis in ("rad", "azi"):
        count = lax.axis_size(axis)
        step = 1
        while step < count:
            x = x + lax.ppermute(x, axis, [(i, i ^ step) for i in range(count)])
            step *= 2
    return x


def with_halo(cells, sides, width, closed):
    for axis, dim in sides:
        count = lax.axis_size(axis)
        ends = count if closed else count - 1
        head = lax.slice_in_dim(cells, 0, width, axis=dim)
        tail = lax.slice_in_dim(cells, cells.shape[dim] - width, cells.shape[dim], axis=dim)
        cells = jnp.concatenate(
            [
                lax.ppermute(tail, axis, [(i, (i + 1) % count) for i in range(ends)]),
                cells,
                lax.ppermute(head, axis, [((i + 1) % count, i) for i in range(ends)]),
            ],
            axis=dim,
        )
    return cells


def mm(spec, a, b):
    return jnp.einsum(spec, a, b, precision=lax.Precision.HIGHEST,
                      preferred_element_type=jnp.float32)


def on_device(jacobian, new_block, kept, columns):
    rows_r = new_block.shape[0]
    rows_a = new_block.shape[1]
    elements = rows_r * rows_a
    total_rows = elements * BLK * lax.axis_size("rad") * lax.axis_size("azi")
    kept_flat = kept.reshape(elements, KEEP, BLK)

    kept_gram = all_sum(mm("epi,eqi->pq", kept_flat, kept_flat))

    widened = with_halo(new_block, (("azi", 1),), 1, True)
    padded = with_halo(widened, (("rad", 0),), 1, False)
    shifted = [padded[c // 3 : c // 3 + rows_r, c % 3 : c % 3 + rows_a] for c in range(9)]
    slots = []
    for k in range(5):
        code = columns[:, :, k][:, :, None, None]
        pick = shifted[0]
        for c in range(1, 9):
            pick = jnp.where(code == c, shifted[c], pick)
        slots.append(pick)
    picked = jnp.stack(slots, axis=2)
    image = jnp.einsum("rakij,rakvj->ravi", jacobian, picked, preferred_element_type=jnp.float32)
    image = image.reshape(elements, NEW, BLK)

    moments = all_sum(
        jnp.concatenate([mm("epi,evi->pv", kept_flat, image), mm("evi,ewi->vw", image, image)], axis=0)
    )
    first, image_gram = moments[:KEEP], moments[KEEP:]
    second = first - mm("pq,qv->pv", kept_gram, first)
    coefficients = first + second
    twice = image - mm("epi,pv->evi", kept_flat, coefficients)

    cross = mm("pv,pw->vw", coefficients, first)
    expanded = (
        image_gram - cross - cross.T
        + mm("pv,pw->vw", coefficients, mm("pq,qw->pw", kept_gram, coefficients))
    ) / total_rows
    kept_share = jnp.diagonal(expanded) * 16.0 >= jnp.diagonal(image_gram) / total_rows
    gram = lax.cond(
        jnp.all(kept_share),
        lambda: expanded,
        lambda: all_sum(mm("evi,ewi->vw", twice, twice)) / total_rows,
    )
    lower = jnp.linalg.cholesky(gram)
    flat = jnp.moveaxis(twice, 1, 0).reshape(NEW, elements * BLK)
    solved = lax.linalg.triangular_solve(lower, flat, left_side=True, lower=True)
    basis = jnp.moveaxis(solved.reshape(NEW, elements, BLK), 0, 1).reshape(rows_r, rows_a, NEW, BLK)
    return (basis, coefficients, lower.T)


def solution(mesh):
    return jax.shard_map(
        on_device,
        mesh=mesh,
        in_specs=(
            P("rad", "azi", None, None, None),
            P("rad", "azi", None, None),
            P("rad", "azi", None, None),
            P("rad", "azi", None),
        ),
        out_specs=(P("rad", "azi", None, None), P(), P()),
        check_vma=False,
    )
```

```python
import jax
import jax.numpy as jnp
from jax import lax
from jax.sharding import PartitionSpec as P

BLK = 128
NEW = 32
KEEP = 192
PIECE = 64


def rounds():
    out = []
    for axis in ("rad", "azi"):
        step = 1
        while step < lax.axis_size(axis):
            out.append((axis, step))
            step *= 2
    return out


def all_sum(x, steps):
    for axis, step in steps:
        count = lax.axis_size(axis)
        x = x + lax.ppermute(x, axis, [(i, i ^ step) for i in range(count)])
    return x


def upper_pieces():
    n = KEEP // PIECE
    return [(i, j) for i in range(n) for j in range(i, n)]


def pack_symmetric(g):
    blocks = [g[i * PIECE : (i + 1) * PIECE, j * PIECE : (j + 1) * PIECE] for i, j in upper_pieces()]
    return jnp.stack(blocks).reshape(-1, BLK)


def unpack_symmetric(flat):
    n = KEEP // PIECE
    blocks = dict(zip(upper_pieces(), flat.reshape(-1, PIECE, PIECE)))
    rows = [
        jnp.concatenate([blocks[(i, j)] if i <= j else blocks[(j, i)].T for j in range(n)], axis=1)
        for i in range(n)
    ]
    return jnp.concatenate(rows, axis=0)


def with_halo(cells, sides, width, closed):
    for axis, dim in sides:
        count = lax.axis_size(axis)
        ends = count if closed else count - 1
        head = lax.slice_in_dim(cells, 0, width, axis=dim)
        tail = lax.slice_in_dim(cells, cells.shape[dim] - width, cells.shape[dim], axis=dim)
        cells = jnp.concatenate(
            [
                lax.ppermute(tail, axis, [(i, (i + 1) % count) for i in range(ends)]),
                cells,
                lax.ppermute(head, axis, [((i + 1) % count, i) for i in range(ends)]),
            ],
            axis=dim,
        )
    return cells


def mm(spec, a, b):
    return jnp.einsum(spec, a, b, precision=lax.Precision.HIGHEST,
                      preferred_element_type=jnp.float32)


def on_device(jacobian, new_block, kept, columns):
    rows_r = new_block.shape[0]
    rows_a = new_block.shape[1]
    elements = rows_r * rows_a
    total_rows = elements * BLK * lax.axis_size("rad") * lax.axis_size("azi")
    kept_flat = kept.reshape(elements, KEEP, BLK)
    steps = rounds()
    ahead = 2

    kept_gram = all_sum(pack_symmetric(mm("epi,eqi->pq", kept_flat, kept_flat)), steps[:ahead])

    widened = with_halo(new_block, (("azi", 1),), 1, True)
    padded = with_halo(widened, (("rad", 0),), 1, False)
    shifted = [padded[c // 3 : c // 3 + rows_r, c % 3 : c % 3 + rows_a] for c in range(9)]
    slots = []
    for k in range(5):
        code = columns[:, :, k][:, :, None, None]
        pick = shifted[0]
        for c in range(1, 9):
            pick = jnp.where(code == c, shifted[c], pick)
        slots.append(pick)
    picked = jnp.stack(slots, axis=2)
    image = jnp.einsum("rakij,rakvj->ravi", jacobian, picked, preferred_element_type=jnp.float32)
    image = image.reshape(elements, NEW, BLK)

    moments = jnp.concatenate(
        [mm("epi,evi->pv", kept_flat, image), mm("evi,ewi->vw", image, image)], axis=0
    ).reshape(-1, BLK)
    split = kept_gram.shape[0]
    joint = all_sum(jnp.concatenate([kept_gram, moments], axis=0), steps[ahead:])
    kept_gram = unpack_symmetric(joint[:split])
    moments = all_sum(joint[split:], steps[:ahead]).reshape(KEEP + NEW, NEW)
    first, image_gram = moments[:KEEP], moments[KEEP:]

    second = first - mm("pq,qv->pv", kept_gram, first)
    coefficients = first + second
    twice = image - mm("epi,pv->evi", kept_flat, coefficients)

    cross = mm("pv,pw->vw", coefficients, first)
    expanded = (
        image_gram - cross - cross.T
        + mm("pv,pw->vw", coefficients, mm("pq,qw->pw", kept_gram, coefficients))
    ) / total_rows
    eye = jnp.eye(NEW, dtype=jnp.float32)
    kept_share = jnp.sum(expanded * eye, axis=1) * 16.0 >= jnp.sum(image_gram * eye, axis=1) / total_rows
    gram = lax.cond(
        jnp.all(kept_share),
        lambda: expanded,
        lambda: all_sum(mm("evi,ewi->vw", twice, twice), steps) / total_rows,
    )
    lower = jnp.linalg.cholesky(gram)
    flat = jnp.moveaxis(twice, 1, 0).reshape(NEW, elements * BLK)
    solved = lax.linalg.triangular_solve(lower, flat, left_side=True, lower=True)
    basis = jnp.moveaxis(solved.reshape(NEW, elements, BLK), 0, 1).reshape(rows_r, rows_a, NEW, BLK)
    return (basis, coefficients, lower.T)


def solution(mesh):
    return jax.shard_map(
        on_device,
        mesh=mesh,
        in_specs=(
            P("rad", "azi", None, None, None),
            P("rad", "azi", None, None),
            P("rad", "azi", None, None),
            P("rad", "azi", None),
        ),
        out_specs=(P("rad", "azi", None, None), P(), P()),
        check_vma=False,
    )
```

```python
import jax
import jax.numpy as jnp
from jax import lax
from jax.sharding import PartitionSpec as P

BLK = 128
NEW = 32
KEEP = 192


def rounds():
    out = []
    for axis in ("rad", "azi"):
        step = 1
        while step < lax.axis_size(axis):
            out.append((axis, step))
            step *= 2
    return out


def all_sum(x, steps):
    for axis, step in steps:
        count = lax.axis_size(axis)
        x = x + lax.ppermute(x, axis, [(i, i ^ step) for i in range(count)])
    return x


def pack_symmetric(g):
    return jnp.concatenate([g[:, :BLK], g[BLK:, BLK:].reshape(-1, BLK)], axis=0)


def apply_symmetric(packed, x):
    tail = KEEP - BLK
    upper, lower = packed[:BLK], packed[BLK:KEEP]
    corner = packed[KEEP:].reshape(tail, tail)
    head, rest = x[:BLK], x[BLK:]
    return jnp.concatenate(
        [mm("pq,qv->pv", upper, head) + mm("qp,qv->pv", lower, rest),
         mm("pq,qv->pv", lower, head) + mm("pq,qv->pv", corner, rest)],
        axis=0,
    )


def with_halo(cells, sides, width, closed):
    for axis, dim in sides:
        count = lax.axis_size(axis)
        ends = count if closed else count - 1
        head = lax.slice_in_dim(cells, 0, width, axis=dim)
        tail = lax.slice_in_dim(cells, cells.shape[dim] - width, cells.shape[dim], axis=dim)
        cells = jnp.concatenate(
            [
                lax.ppermute(tail, axis, [(i, (i + 1) % count) for i in range(ends)]),
                cells,
                lax.ppermute(head, axis, [((i + 1) % count, i) for i in range(ends)]),
            ],
            axis=dim,
        )
    return cells


def mm(spec, a, b):
    return jnp.einsum(spec, a, b, precision=lax.Precision.HIGHEST,
                      preferred_element_type=jnp.float32)


def on_device(jacobian, new_block, kept, columns):
    rows_r = new_block.shape[0]
    rows_a = new_block.shape[1]
    elements = rows_r * rows_a
    total_rows = elements * BLK * lax.axis_size("rad") * lax.axis_size("azi")
    kept_flat = kept.reshape(elements, KEEP, BLK)
    steps = rounds()
    ahead = 4

    kept_gram = all_sum(pack_symmetric(mm("epi,eqi->pq", kept_flat, kept_flat)), steps[:ahead])

    widened = with_halo(new_block, (("azi", 1),), 1, True)
    padded = with_halo(widened, (("rad", 0),), 1, False)
    shifted = [padded[c // 3 : c // 3 + rows_r, c % 3 : c % 3 + rows_a] for c in range(9)]
    slots = []
    for k in range(5):
        code = columns[:, :, k][:, :, None, None]
        pick = shifted[0]
        for c in range(1, 9):
            pick = jnp.where(code == c, shifted[c], pick)
        slots.append(pick)
    picked = jnp.stack(slots, axis=2)
    image = jnp.einsum("rakij,rakvj->ravi", jacobian, picked, preferred_element_type=jnp.float32)
    image = image.reshape(elements, NEW, BLK)

    moments = jnp.concatenate(
        [mm("epi,evi->pv", kept_flat, image), mm("evi,ewi->vw", image, image)], axis=0
    ).reshape(-1, BLK)
    split = kept_gram.shape[0]
    joint = all_sum(jnp.concatenate([kept_gram, moments], axis=0), steps[ahead:])
    kept_gram = joint[:split]
    moments = all_sum(joint[split:], steps[:ahead]).reshape(KEEP + NEW, NEW)
    first, image_gram = moments[:KEEP], moments[KEEP:]

    second = first - apply_symmetric(kept_gram, first)
    coefficients = first + second
    twice = image - mm("epi,pv->evi", kept_flat, coefficients)

    cross = mm("pv,pw->vw", coefficients, first)
    expanded = (
        image_gram - cross - cross.T
        + mm("pv,pw->vw", coefficients, apply_symmetric(kept_gram, coefficients))
    ) / total_rows
    eye = jnp.eye(NEW, dtype=jnp.float32)
    kept_share = jnp.sum(expanded * eye, axis=1) * 16.0 >= jnp.sum(image_gram * eye, axis=1) / total_rows
    gram = lax.cond(
        jnp.all(kept_share),
        lambda: expanded,
        lambda: all_sum(mm("evi,ewi->vw", twice, twice), steps) / total_rows,
    )
    lower = jnp.linalg.cholesky(gram)
    flat = jnp.moveaxis(twice, 1, 0).reshape(NEW, elements * BLK)
    solved = lax.linalg.triangular_solve(lower, flat, left_side=True, lower=True)
    basis = jnp.moveaxis(solved.reshape(NEW, elements, BLK), 0, 1).reshape(rows_r, rows_a, NEW, BLK)
    return (basis, coefficients, lower.T)


def solution(mesh):
    return jax.shard_map(
        on_device,
        mesh=mesh,
        in_specs=(
            P("rad", "azi", None, None, None),
            P("rad", "azi", None, None),
            P("rad", "azi", None, None),
            P("rad", "azi", None),
        ),
        out_specs=(P("rad", "azi", None, None), P(), P()),
        check_vma=False,
    )
```

```python
import jax
import jax.numpy as jnp
from jax import lax
from jax.sharding import PartitionSpec as P

BLK = 128
NEW = 32
KEEP = 192


def rounds():
    out = []
    for axis in ("rad", "azi"):
        step = 1
        while step < lax.axis_size(axis):
            out.append((axis, step))
            step *= 2
    return out


def all_sum(x, steps):
    for axis, step in steps:
        count = lax.axis_size(axis)
        x = x + lax.ppermute(x, axis, [(i, i ^ step) for i in range(count)])
    return x


def exchange(x, axis, step):
    count = lax.axis_size(axis)
    return lax.ppermute(x, axis, [(i, i ^ step) for i in range(count)])


def upper_bit(axis, step):
    return (lax.axis_index(axis) // step) % 2 == 1


def halve(x, axis, step):
    half = x.shape[0] // 2
    lo, hi = x[:half], x[half:]
    bit = upper_bit(axis, step)
    return jnp.where(bit, hi, lo) + exchange(jnp.where(bit, lo, hi), axis, step)


def join(mine, other, axis, step):
    return jnp.where(
        upper_bit(axis, step),
        jnp.concatenate([other, mine], axis=0),
        jnp.concatenate([mine, other], axis=0),
    )


def pack_symmetric(g):
    return jnp.concatenate([g[:, :BLK], g[BLK:, BLK:].reshape(-1, BLK)], axis=0)


def unpack_symmetric(packed):
    tail = KEEP - BLK
    upper, lower = packed[:BLK], packed[BLK:KEEP]
    corner = packed[KEEP:].reshape(tail, tail)
    return jnp.concatenate(
        [jnp.concatenate([upper, lower.T], axis=1), jnp.concatenate([lower, corner], axis=1)], axis=0
    )


def with_halo(cells, sides, width, closed):
    for axis, dim in sides:
        count = lax.axis_size(axis)
        ends = count if closed else count - 1
        head = lax.slice_in_dim(cells, 0, width, axis=dim)
        tail = lax.slice_in_dim(cells, cells.shape[dim] - width, cells.shape[dim], axis=dim)
        cells = jnp.concatenate(
            [
                lax.ppermute(tail, axis, [(i, (i + 1) % count) for i in range(ends)]),
                cells,
                lax.ppermute(head, axis, [((i + 1) % count, i) for i in range(ends)]),
            ],
            axis=dim,
        )
    return cells


def mm(spec, a, b):
    return jnp.einsum(spec, a, b, precision=lax.Precision.HIGHEST,
                      preferred_element_type=jnp.float32)


def on_device(jacobian, new_block, kept, columns):
    rows_r = new_block.shape[0]
    rows_a = new_block.shape[1]
    elements = rows_r * rows_a
    total_rows = elements * BLK * lax.axis_size("rad") * lax.axis_size("azi")
    kept_flat = kept.reshape(elements, KEEP, BLK)
    steps = rounds()
    radial = [step for axis, step in steps if axis == "rad"]
    around = [("azi", step) for axis, step in steps if axis == "azi"]

    kept_gram = pack_symmetric(mm("epi,eqi->pq", kept_flat, kept_flat))
    for step in radial:
        kept_gram = halve(kept_gram, "rad", step)

    widened = with_halo(new_block, (("azi", 1),), 1, True)
    padded = with_halo(widened, (("rad", 0),), 1, False)
    shifted = [padded[c // 3 : c // 3 + rows_r, c % 3 : c % 3 + rows_a] for c in range(9)]
    slots = []
    for k in range(5):
        code = columns[:, :, k][:, :, None, None]
        pick = shifted[0]
        for c in range(1, 9):
            pick = jnp.where(code == c, shifted[c], pick)
        slots.append(pick)
    picked = jnp.stack(slots, axis=2)
    image = jnp.einsum("rakij,rakvj->ravi", jacobian, picked, preferred_element_type=jnp.float32)
    image = image.reshape(elements, NEW, BLK)

    moments = jnp.concatenate(
        [mm("epi,evi->pv", kept_flat, image), mm("evi,ewi->vw", image, image)], axis=0
    ).reshape(-1, BLK)
    split = kept_gram.shape[0]
    joint = all_sum(jnp.concatenate([kept_gram, moments], axis=0), around)
    kept_gram, moments = joint[:split], joint[split:]
    for step in reversed(radial):
        other = exchange(jnp.concatenate([kept_gram, moments], axis=0), "rad", step)
        moments = moments + other[kept_gram.shape[0]:]
        kept_gram = join(kept_gram, other[: kept_gram.shape[0]], "rad", step)
    kept_gram = unpack_symmetric(kept_gram)
    moments = moments.reshape(KEEP + NEW, NEW)
    first, image_gram = moments[:KEEP], moments[KEEP:]

    second = first - mm("pq,qv->pv", kept_gram, first)
    coefficients = first + second
    twice = image - mm("epi,pv->evi", kept_flat, coefficients)

    cross = mm("pv,pw->vw", coefficients, first)
    expanded = (
        image_gram - cross - cross.T
        + mm("pv,pw->vw", coefficients, mm("pq,qw->pw", kept_gram, coefficients))
    ) / total_rows
    eye = jnp.eye(NEW, dtype=jnp.float32)
    kept_share = jnp.sum(expanded * eye, axis=1) * 16.0 >= jnp.sum(image_gram * eye, axis=1) / total_rows
    gram = lax.cond(
        jnp.all(kept_share),
        lambda: expanded,
        lambda: all_sum(mm("evi,ewi->vw", twice, twice), steps) / total_rows,
    )
    lower = jnp.linalg.cholesky(gram)
    flat = jnp.moveaxis(twice, 1, 0).reshape(NEW, elements * BLK)
    solved = lax.linalg.triangular_solve(lower, flat, left_side=True, lower=True)
    basis = jnp.moveaxis(solved.reshape(NEW, elements, BLK), 0, 1).reshape(rows_r, rows_a, NEW, BLK)
    return (basis, coefficients, lower.T)


def solution(mesh):
    return jax.shard_map(
        on_device,
        mesh=mesh,
        in_specs=(
            P("rad", "azi", None, None, None),
            P("rad", "azi", None, None),
            P("rad", "azi", None, None),
            P("rad", "azi", None),
        ),
        out_specs=(P("rad", "azi", None, None), P(), P()),
        check_vma=False,
    )
```

```python
import jax
import jax.numpy as jnp
from jax import lax
from jax.sharding import PartitionSpec as P

BLK = 128
NEW = 32
KEEP = 192


def rounds():
    out = []
    for axis in ("rad", "azi"):
        step = 1
        while step < lax.axis_size(axis):
            out.append((axis, step))
            step *= 2
    return out


def all_sum(x, steps):
    for axis, step in steps:
        count = lax.axis_size(axis)
        x = x + lax.ppermute(x, axis, [(i, i ^ step) for i in range(count)])
    return x


def exchange(x, axis, step):
    count = lax.axis_size(axis)
    return lax.ppermute(x, axis, [(i, i ^ step) for i in range(count)])


def upper_bit(axis, step):
    return (lax.axis_index(axis) // step) % 2 == 1


def halve(x, axis, step):
    half = x.shape[0] // 2
    lo, hi = x[:half], x[half:]
    bit = upper_bit(axis, step)
    return jnp.where(bit, hi, lo) + exchange(jnp.where(bit, lo, hi), axis, step)


def join(mine, other, axis, step):
    return jnp.where(
        upper_bit(axis, step),
        jnp.concatenate([other, mine], axis=0),
        jnp.concatenate([mine, other], axis=0),
    )


def pack_symmetric(g):
    return jnp.concatenate([g[:, :BLK], g[BLK:, BLK:].reshape(-1, BLK)], axis=0)


def unpack_symmetric(packed):
    tail = KEEP - BLK
    upper, lower = packed[:BLK], packed[BLK:KEEP]
    corner = packed[KEEP:].reshape(tail, tail)
    return jnp.concatenate(
        [jnp.concatenate([upper, lower.T], axis=1), jnp.concatenate([lower, corner], axis=1)], axis=0
    )


def with_halo(cells, sides, width, closed):
    for axis, dim in sides:
        count = lax.axis_size(axis)
        ends = count if closed else count - 1
        head = lax.slice_in_dim(cells, 0, width, axis=dim)
        tail = lax.slice_in_dim(cells, cells.shape[dim] - width, cells.shape[dim], axis=dim)
        cells = jnp.concatenate(
            [
                lax.ppermute(tail, axis, [(i, (i + 1) % count) for i in range(ends)]),
                cells,
                lax.ppermute(head, axis, [((i + 1) % count, i) for i in range(ends)]),
            ],
            axis=dim,
        )
    return cells


def mm(spec, a, b):
    return jnp.einsum(spec, a, b, precision=lax.Precision.HIGHEST,
                      preferred_element_type=jnp.float32)


def on_device(jacobian, new_block, kept, columns):
    rows_r = new_block.shape[0]
    rows_a = new_block.shape[1]
    elements = rows_r * rows_a
    total_rows = elements * BLK * lax.axis_size("rad") * lax.axis_size("azi")
    kept_flat = kept.reshape(elements, KEEP, BLK)
    steps = rounds()
    radial = [step for axis, step in steps if axis == "rad"]
    around = [("azi", step) for axis, step in steps if axis == "azi"]

    kept_gram = halve(pack_symmetric(mm("epi,eqi->pq", kept_flat, kept_flat)), "rad", radial[0])

    widened = with_halo(new_block, (("azi", 1),), 1, True)
    padded = with_halo(widened, (("rad", 0),), 1, False)
    kept_gram, padded = lax.optimization_barrier((kept_gram, padded))
    kept_gram = halve(kept_gram, "rad", radial[1])
    shifted = [padded[c // 3 : c // 3 + rows_r, c % 3 : c % 3 + rows_a] for c in range(9)]
    slots = []
    for k in range(5):
        code = columns[:, :, k][:, :, None, None]
        pick = shifted[0]
        for c in range(1, 9):
            pick = jnp.where(code == c, shifted[c], pick)
        slots.append(pick)
    picked = jnp.stack(slots, axis=2)
    kept_gram, picked = lax.optimization_barrier((kept_gram, picked))
    kept_gram = halve(kept_gram, "rad", radial[2])
    image = jnp.einsum("rakij,rakvj->ravi", jacobian, picked, preferred_element_type=jnp.float32)
    image = image.reshape(elements, NEW, BLK)
    kept_gram, image = lax.optimization_barrier((kept_gram, image))
    kept_gram = halve(kept_gram, "rad", radial[3])

    moments = jnp.concatenate(
        [mm("epi,evi->pv", kept_flat, image), mm("evi,ewi->vw", image, image)], axis=0
    ).reshape(-1, BLK)
    split = kept_gram.shape[0]
    joint = all_sum(jnp.concatenate([kept_gram, moments], axis=0), around)
    kept_gram, moments = joint[:split], joint[split:]
    for step in reversed(radial):
        other = exchange(jnp.concatenate([kept_gram, moments], axis=0), "rad", step)
        moments = moments + other[kept_gram.shape[0]:]
        kept_gram = join(kept_gram, other[: kept_gram.shape[0]], "rad", step)
    kept_gram = unpack_symmetric(kept_gram)
    moments = moments.reshape(KEEP + NEW, NEW)
    first, image_gram = moments[:KEEP], moments[KEEP:]

    second = first - mm("pq,qv->pv", kept_gram, first)
    coefficients = first + second
    twice = image - mm("epi,pv->evi", kept_flat, coefficients)

    cross = mm("pv,pw->vw", coefficients, first)
    expanded = (
        image_gram - cross - cross.T
        + mm("pv,pw->vw", coefficients, mm("pq,qw->pw", kept_gram, coefficients))
    ) / total_rows
    eye = jnp.eye(NEW, dtype=jnp.float32)
    kept_share = jnp.sum(expanded * eye, axis=1) * 16.0 >= jnp.sum(image_gram * eye, axis=1) / total_rows
    gram = lax.cond(
        jnp.all(kept_share),
        lambda: expanded,
        lambda: all_sum(mm("evi,ewi->vw", twice, twice), steps) / total_rows,
    )
    lower = jnp.linalg.cholesky(gram)
    flat = jnp.moveaxis(twice, 1, 0).reshape(NEW, elements * BLK)
    solved = lax.linalg.triangular_solve(lower, flat, left_side=True, lower=True)
    basis = jnp.moveaxis(solved.reshape(NEW, elements, BLK), 0, 1).reshape(rows_r, rows_a, NEW, BLK)
    return (basis, coefficients, lower.T)


def solution(mesh):
    return jax.shard_map(
        on_device,
        mesh=mesh,
        in_specs=(
            P("rad", "azi", None, None, None),
            P("rad", "azi", None, None),
            P("rad", "azi", None, None),
            P("rad", "azi", None),
        ),
        out_specs=(P("rad", "azi", None, None), P(), P()),
        check_vma=False,
    )
```

```python
import jax
import jax.numpy as jnp
from jax import lax
from jax.sharding import PartitionSpec as P

BLK = 128
NEW = 32
KEEP = 192


def rounds():
    out = []
    for axis in ("rad", "azi"):
        step = 1
        while step < lax.axis_size(axis):
            out.append((axis, step))
            step *= 2
    return out


def all_sum(x, steps):
    for axis, step in steps:
        count = lax.axis_size(axis)
        x = x + lax.ppermute(x, axis, [(i, i ^ step) for i in range(count)])
    return x


def exchange(x, axis, step):
    count = lax.axis_size(axis)
    return lax.ppermute(x, axis, [(i, i ^ step) for i in range(count)])


def upper_bit(axis, step):
    return (lax.axis_index(axis) // step) % 2 == 1


def halve(x, axis, step):
    half = x.shape[0] // 2
    lo, hi = x[:half], x[half:]
    bit = upper_bit(axis, step)
    return jnp.where(bit, hi, lo) + exchange(jnp.where(bit, lo, hi), axis, step)


def join(mine, other, axis, step):
    return jnp.where(
        upper_bit(axis, step),
        jnp.concatenate([other, mine], axis=0),
        jnp.concatenate([mine, other], axis=0),
    )


def pack_symmetric(g):
    return jnp.concatenate([g[:, :BLK], g[BLK:, BLK:].reshape(-1, BLK)], axis=0)


def unpack_symmetric(packed):
    tail = KEEP - BLK
    upper, lower = packed[:BLK], packed[BLK:KEEP]
    corner = packed[KEEP:].reshape(tail, tail)
    return jnp.concatenate(
        [jnp.concatenate([upper, lower.T], axis=1), jnp.concatenate([lower, corner], axis=1)], axis=0
    )


def with_halo(cells, sides, width, closed):
    for axis, dim in sides:
        count = lax.axis_size(axis)
        ends = count if closed else count - 1
        head = lax.slice_in_dim(cells, 0, width, axis=dim)
        tail = lax.slice_in_dim(cells, cells.shape[dim] - width, cells.shape[dim], axis=dim)
        cells = jnp.concatenate(
            [
                lax.ppermute(tail, axis, [(i, (i + 1) % count) for i in range(ends)]),
                cells,
                lax.ppermute(head, axis, [((i + 1) % count, i) for i in range(ends)]),
            ],
            axis=dim,
        )
    return cells


def mm(spec, a, b):
    return jnp.einsum(spec, a, b, precision=lax.Precision.HIGHEST,
                      preferred_element_type=jnp.float32)


def on_device(jacobian, new_block, kept, columns):
    rows_r = new_block.shape[0]
    rows_a = new_block.shape[1]
    elements = rows_r * rows_a
    total_rows = elements * BLK * lax.axis_size("rad") * lax.axis_size("azi")
    kept_flat = kept.reshape(elements, KEEP, BLK)
    steps = rounds()
    radial = [step for axis, step in steps if axis == "rad"]
    around = [("azi", step) for axis, step in steps if axis == "azi"]

    kept_gram = halve(pack_symmetric(mm("epi,eqi->pq", kept_flat, kept_flat)), "rad", radial[0])

    widened = with_halo(new_block, (("azi", 1),), 1, True)
    padded = with_halo(widened, (("rad", 0),), 1, False)
    kept_gram, padded = lax.optimization_barrier((kept_gram, padded))
    kept_gram = halve(kept_gram, "rad", radial[1])
    shifted = [padded[c // 3 : c // 3 + rows_r, c % 3 : c % 3 + rows_a] for c in range(9)]
    slots = [new_block]
    for k in range(1, 5):
        code = columns[:, :, k][:, :, None, None]
        pick = shifted[0]
        for c in range(1, 9):
            pick = jnp.where(code == c, shifted[c], pick)
        slots.append(pick)
    picked = jnp.stack(slots, axis=2)
    kept_gram, picked = lax.optimization_barrier((kept_gram, picked))
    kept_gram = halve(kept_gram, "rad", radial[2])
    image = jnp.einsum("rakij,rakvj->ravi", jacobian, picked, preferred_element_type=jnp.float32)
    image = image.reshape(elements, NEW, BLK)
    kept_gram, image = lax.optimization_barrier((kept_gram, image))
    kept_gram = halve(kept_gram, "rad", radial[3])

    moments = jnp.concatenate(
        [mm("epi,evi->pv", kept_flat, image), mm("evi,ewi->vw", image, image)], axis=0
    ).reshape(-1, BLK)
    split = kept_gram.shape[0]
    joint = all_sum(jnp.concatenate([kept_gram, moments], axis=0), around)
    kept_gram, moments = joint[:split], joint[split:]
    for step in reversed(radial):
        other = exchange(jnp.concatenate([kept_gram, moments], axis=0), "rad", step)
        moments = moments + other[kept_gram.shape[0]:]
        kept_gram = join(kept_gram, other[: kept_gram.shape[0]], "rad", step)
    kept_gram = unpack_symmetric(kept_gram)
    moments = moments.reshape(KEEP + NEW, NEW)
    first, image_gram = moments[:KEEP], moments[KEEP:]

    second = first - mm("pq,qv->pv", kept_gram, first)
    coefficients = first + second

    cross = mm("pv,pw->vw", coefficients, first)
    expanded = (
        image_gram - cross - cross.T
        + mm("pv,pw->vw", coefficients, mm("pq,qw->pw", kept_gram, coefficients))
    ) / total_rows
    eye = jnp.eye(NEW, dtype=jnp.float32)
    kept_share = jnp.sum(expanded * eye, axis=1) * 16.0 >= jnp.sum(image_gram * eye, axis=1) / total_rows

    def factor_of(gram):
        lower = jnp.linalg.cholesky(gram)
        inverse = lax.linalg.triangular_solve(lower, eye, left_side=True, lower=True)
        return lower, inverse

    def expanded_path():
        lower, inverse = factor_of(expanded)
        basis = mm("evi,wv->ewi", image, inverse) - mm(
            "epi,pw->ewi", kept_flat, mm("pv,wv->pw", coefficients, inverse)
        )
        return basis, lower

    def direct_path():
        twice = image - mm("epi,pv->evi", kept_flat, coefficients)
        lower, inverse = factor_of(all_sum(mm("evi,ewi->vw", twice, twice), steps) / total_rows)
        return mm("evi,wv->ewi", twice, inverse), lower

    basis, lower = lax.cond(jnp.all(kept_share), expanded_path, direct_path)
    basis = basis.reshape(rows_r, rows_a, NEW, BLK)
    return (basis, coefficients, lower.T)


def solution(mesh):
    return jax.shard_map(
        on_device,
        mesh=mesh,
        in_specs=(
            P("rad", "azi", None, None, None),
            P("rad", "azi", None, None),
            P("rad", "azi", None, None),
            P("rad", "azi", None),
        ),
        out_specs=(P("rad", "azi", None, None), P(), P()),
        check_vma=False,
    )
```

```python
import jax
import jax.numpy as jnp
from jax import lax
from jax.sharding import PartitionSpec as P

BLK = 128
NEW = 32
KEEP = 192


def rounds():
    out = []
    for axis in ("rad", "azi"):
        step = 1
        while step < lax.axis_size(axis):
            out.append((axis, step))
            step *= 2
    return out


def all_sum(x, steps):
    for axis, step in steps:
        count = lax.axis_size(axis)
        x = x + lax.ppermute(x, axis, [(i, i ^ step) for i in range(count)])
    return x


def exchange(x, axis, step):
    count = lax.axis_size(axis)
    return lax.ppermute(x, axis, [(i, i ^ step) for i in range(count)])


def upper_bit(axis, step):
    return (lax.axis_index(axis) // step) % 2 == 1


def halve(x, axis, step):
    half = x.shape[0] // 2
    lo, hi = x[:half], x[half:]
    bit = upper_bit(axis, step)
    return jnp.where(bit, hi, lo) + exchange(jnp.where(bit, lo, hi), axis, step)


def join(mine, other, axis, step):
    return jnp.where(
        upper_bit(axis, step),
        jnp.concatenate([other, mine], axis=0),
        jnp.concatenate([mine, other], axis=0),
    )


def pack_symmetric(g):
    return jnp.concatenate([g[:, :BLK], g[BLK:, BLK:].reshape(-1, BLK)], axis=0)


def unpack_symmetric(packed):
    tail = KEEP - BLK
    upper, lower = packed[:BLK], packed[BLK:KEEP]
    corner = packed[KEEP:].reshape(tail, tail)
    return jnp.concatenate(
        [jnp.concatenate([upper, lower.T], axis=1), jnp.concatenate([lower, corner], axis=1)], axis=0
    )


def with_halo(cells, sides, width, closed):
    for axis, dim in sides:
        count = lax.axis_size(axis)
        ends = count if closed else count - 1
        head = lax.slice_in_dim(cells, 0, width, axis=dim)
        tail = lax.slice_in_dim(cells, cells.shape[dim] - width, cells.shape[dim], axis=dim)
        cells = jnp.concatenate(
            [
                lax.ppermute(tail, axis, [(i, (i + 1) % count) for i in range(ends)]),
                cells,
                lax.ppermute(head, axis, [((i + 1) % count, i) for i in range(ends)]),
            ],
            axis=dim,
        )
    return cells


def mm(spec, a, b):
    return jnp.einsum(spec, a, b, precision=lax.Precision.HIGHEST,
                      preferred_element_type=jnp.float32)


def on_device(jacobian, new_block, kept, columns):
    rows_r = new_block.shape[0]
    rows_a = new_block.shape[1]
    elements = rows_r * rows_a
    total_rows = elements * BLK * lax.axis_size("rad") * lax.axis_size("azi")
    kept_flat = kept.reshape(elements, KEEP, BLK)
    steps = rounds()
    radial = [step for axis, step in steps if axis == "rad"]
    around = [("azi", step) for axis, step in steps if axis == "azi"]

    kept_gram = halve(pack_symmetric(mm("epi,eqi->pq", kept_flat, kept_flat)), "rad", radial[0])

    n_a, n_r = lax.axis_size("azi"), lax.axis_size("rad")
    west = lax.ppermute(new_block[:, rows_a - 1 :], "azi", [(i, (i + 1) % n_a) for i in range(n_a)])
    east = lax.ppermute(new_block[:, :1], "azi", [((i + 1) % n_a, i) for i in range(n_a)])
    kept_gram, west, east = lax.optimization_barrier((kept_gram, west, east))
    kept_gram = halve(kept_gram, "rad", radial[1])

    def row(r):
        return jnp.concatenate([west[r : r + 1], new_block[r : r + 1], east[r : r + 1]], axis=1)

    north = lax.ppermute(row(rows_r - 1), "rad", [(i, i + 1) for i in range(n_r - 1)])
    south = lax.ppermute(row(0), "rad", [(i + 1, i) for i in range(n_r - 1)])
    padded = jnp.concatenate(
        [north, jnp.concatenate([west, new_block, east], axis=1), south], axis=0
    )
    shifted = [padded[c // 3 : c // 3 + rows_r, c % 3 : c % 3 + rows_a] for c in range(9)]
    slots = [new_block]
    for k in range(1, 5):
        code = columns[:, :, k][:, :, None, None]
        pick = shifted[0]
        for c in range(1, 9):
            pick = jnp.where(code == c, shifted[c], pick)
        slots.append(pick)
    picked = jnp.stack(slots, axis=2)
    image = jnp.einsum("rakij,rakvj->ravi", jacobian, picked, preferred_element_type=jnp.float32)
    image = image.reshape(elements, NEW, BLK)

    moments = jnp.concatenate(
        [mm("epi,evi->pv", kept_flat, image), mm("evi,ewi->vw", image, image)], axis=0
    ).reshape(-1, BLK)
    split = kept_gram.shape[0]
    ahead = 2
    joint = all_sum(
        jnp.concatenate([kept_gram, moments], axis=0),
        [("rad", step) for step in radial[ahead:]] + around,
    )
    kept_gram, moments = joint[:split], joint[split:]
    for step in reversed(radial[:ahead]):
        other = exchange(jnp.concatenate([kept_gram, moments], axis=0), "rad", step)
        moments = moments + other[kept_gram.shape[0]:]
        kept_gram = join(kept_gram, other[: kept_gram.shape[0]], "rad", step)
    kept_gram = unpack_symmetric(kept_gram)
    moments = moments.reshape(KEEP + NEW, NEW)
    first, image_gram = moments[:KEEP], moments[KEEP:]

    second = first - mm("pq,qv->pv", kept_gram, first)
    coefficients = first + second

    cross = mm("pv,pw->vw", coefficients, first)
    expanded = (
        image_gram - cross - cross.T
        + mm("pv,pw->vw", coefficients, mm("pq,qw->pw", kept_gram, coefficients))
    ) / total_rows
    eye = jnp.eye(NEW, dtype=jnp.float32)
    kept_share = jnp.sum(expanded * eye, axis=1) * 16.0 >= jnp.sum(image_gram * eye, axis=1) / total_rows

    def factor_of(gram):
        lower = jnp.linalg.cholesky(gram)
        inverse = lax.linalg.triangular_solve(lower, eye, left_side=True, lower=True)
        return lower, inverse

    def expanded_path():
        lower, inverse = factor_of(expanded)
        basis = mm("evi,wv->ewi", image, inverse) - mm(
            "epi,pw->ewi", kept_flat, mm("pv,wv->pw", coefficients, inverse)
        )
        return basis, lower

    def direct_path():
        twice = image - mm("epi,pv->evi", kept_flat, coefficients)
        lower, inverse = factor_of(all_sum(mm("evi,ewi->vw", twice, twice), steps) / total_rows)
        return mm("evi,wv->ewi", twice, inverse), lower

    basis, lower = lax.cond(jnp.all(kept_share), expanded_path, direct_path)
    basis = basis.reshape(rows_r, rows_a, NEW, BLK)
    return (basis, coefficients, lower.T)


def solution(mesh):
    return jax.shard_map(
        on_device,
        mesh=mesh,
        in_specs=(
            P("rad", "azi", None, None, None),
            P("rad", "azi", None, None),
            P("rad", "azi", None, None),
            P("rad", "azi", None),
        ),
        out_specs=(P("rad", "azi", None, None), P(), P()),
        check_vma=False,
    )
```

```python
import jax
import jax.numpy as jnp
from jax import lax
from jax.sharding import PartitionSpec as P

BLK = 128
NEW = 32
KEEP = 192


def rounds():
    out = []
    for axis in ("rad", "azi"):
        step = 1
        while step < lax.axis_size(axis):
            out.append((axis, step))
            step *= 2
    return out


def all_sum(x, steps):
    for axis, step in steps:
        count = lax.axis_size(axis)
        x = x + lax.ppermute(x, axis, [(i, i ^ step) for i in range(count)])
    return x


def exchange(x, axis, step):
    count = lax.axis_size(axis)
    return lax.ppermute(x, axis, [(i, i ^ step) for i in range(count)])


def upper_bit(axis, step):
    return (lax.axis_index(axis) // step) % 2 == 1


def halve(x, axis, step):
    half = x.shape[0] // 2
    lo, hi = x[:half], x[half:]
    bit = upper_bit(axis, step)
    return jnp.where(bit, hi, lo) + exchange(jnp.where(bit, lo, hi), axis, step)


def join(mine, other, axis, step):
    return jnp.where(
        upper_bit(axis, step),
        jnp.concatenate([other, mine], axis=0),
        jnp.concatenate([mine, other], axis=0),
    )


def pack_symmetric(g):
    return jnp.concatenate([g[:, :BLK], g[BLK:, BLK:].reshape(-1, BLK)], axis=0)


def unpack_symmetric(packed):
    tail = KEEP - BLK
    upper, lower = packed[:BLK], packed[BLK:KEEP]
    corner = packed[KEEP:].reshape(tail, tail)
    return jnp.concatenate(
        [jnp.concatenate([upper, lower.T], axis=1), jnp.concatenate([lower, corner], axis=1)], axis=0
    )


def with_halo(cells, sides, width, closed):
    for axis, dim in sides:
        count = lax.axis_size(axis)
        ends = count if closed else count - 1
        head = lax.slice_in_dim(cells, 0, width, axis=dim)
        tail = lax.slice_in_dim(cells, cells.shape[dim] - width, cells.shape[dim], axis=dim)
        cells = jnp.concatenate(
            [
                lax.ppermute(tail, axis, [(i, (i + 1) % count) for i in range(ends)]),
                cells,
                lax.ppermute(head, axis, [((i + 1) % count, i) for i in range(ends)]),
            ],
            axis=dim,
        )
    return cells


def mm(spec, a, b):
    return jnp.einsum(spec, a, b, precision=lax.Precision.HIGHEST,
                      preferred_element_type=jnp.float32)


def on_device(jacobian, new_block, kept, columns):
    rows_r = new_block.shape[0]
    rows_a = new_block.shape[1]
    elements = rows_r * rows_a
    total_rows = elements * BLK * lax.axis_size("rad") * lax.axis_size("azi")
    kept_flat = kept.reshape(elements, KEEP, BLK)
    steps = rounds()
    radial = [step for axis, step in steps if axis == "rad"]
    around = [("azi", step) for axis, step in steps if axis == "azi"]

    kept_gram = halve(pack_symmetric(jnp.einsum(
        "epi,eqi->pq", kept_flat, kept_flat, precision=lax.Precision.HIGH,
        preferred_element_type=jnp.float32)), "rad", radial[0])

    n_a, n_r = lax.axis_size("azi"), lax.axis_size("rad")
    west = lax.ppermute(new_block[:, rows_a - 1 :], "azi", [(i, (i + 1) % n_a) for i in range(n_a)])
    east = lax.ppermute(new_block[:, :1], "azi", [((i + 1) % n_a, i) for i in range(n_a)])
    kept_gram, west, east = lax.optimization_barrier((kept_gram, west, east))
    kept_gram = halve(kept_gram, "rad", radial[1])

    def row(r):
        return jnp.concatenate([west[r : r + 1], new_block[r : r + 1], east[r : r + 1]], axis=1)

    north = lax.ppermute(row(rows_r - 1), "rad", [(i, i + 1) for i in range(n_r - 1)])
    south = lax.ppermute(row(0), "rad", [(i + 1, i) for i in range(n_r - 1)])
    padded = jnp.concatenate(
        [north, jnp.concatenate([west, new_block, east], axis=1), south], axis=0
    )
    shifted = [padded[c // 3 : c // 3 + rows_r, c % 3 : c % 3 + rows_a] for c in range(9)]
    slots = [new_block]
    for k in range(1, 5):
        code = columns[:, :, k][:, :, None, None]
        pick = shifted[0]
        for c in range(1, 9):
            pick = jnp.where(code == c, shifted[c], pick)
        slots.append(pick)
    picked = jnp.stack(slots, axis=2)
    image = jnp.einsum("rakij,rakvj->ravi", jacobian, picked, preferred_element_type=jnp.float32)
    image = image.reshape(elements, NEW, BLK)

    moments = jnp.concatenate(
        [mm("epi,evi->pv", kept_flat, image), mm("evi,ewi->vw", image, image)], axis=0
    ).reshape(-1, BLK)
    split = kept_gram.shape[0]
    ahead = 2
    joint = all_sum(
        jnp.concatenate([kept_gram, moments], axis=0),
        [("rad", step) for step in radial[ahead:]] + around,
    )
    kept_gram, moments = joint[:split], joint[split:]
    for step in reversed(radial[:ahead]):
        other = exchange(jnp.concatenate([kept_gram, moments], axis=0), "rad", step)
        moments = moments + other[kept_gram.shape[0]:]
        kept_gram = join(kept_gram, other[: kept_gram.shape[0]], "rad", step)
    kept_gram = unpack_symmetric(kept_gram)
    moments = moments.reshape(KEEP + NEW, NEW)
    first, image_gram = moments[:KEEP], moments[KEEP:]

    second = first - mm("pq,qv->pv", kept_gram, first)
    coefficients = first + second

    cross = mm("pv,pw->vw", coefficients, first)
    expanded = (
        image_gram - cross - cross.T
        + mm("pv,pw->vw", coefficients, mm("pq,qw->pw", kept_gram, coefficients))
    ) / total_rows
    eye = jnp.eye(NEW, dtype=jnp.float32)
    kept_share = jnp.sum(expanded * eye, axis=1) * 16.0 >= jnp.sum(image_gram * eye, axis=1) / total_rows

    def factor_of(gram):
        lower = jnp.linalg.cholesky(gram)
        inverse = lax.linalg.triangular_solve(lower, eye, left_side=True, lower=True)
        return lower, inverse

    def expanded_path():
        lower, inverse = factor_of(expanded)
        basis = mm("evi,wv->ewi", image, inverse) - mm(
            "epi,pw->ewi", kept_flat, mm("pv,wv->pw", coefficients, inverse)
        )
        return basis, lower

    def direct_path():
        twice = image - mm("epi,pv->evi", kept_flat, coefficients)
        lower, inverse = factor_of(all_sum(mm("evi,ewi->vw", twice, twice), steps) / total_rows)
        return mm("evi,wv->ewi", twice, inverse), lower

    basis, lower = lax.cond(jnp.all(kept_share), expanded_path, direct_path)
    basis = basis.reshape(rows_r, rows_a, NEW, BLK)
    return (basis, coefficients, lower.T)


def solution(mesh):
    return jax.shard_map(
        on_device,
        mesh=mesh,
        in_specs=(
            P("rad", "azi", None, None, None),
            P("rad", "azi", None, None),
            P("rad", "azi", None, None),
            P("rad", "azi", None),
        ),
        out_specs=(P("rad", "azi", None, None), P(), P()),
        check_vma=False,
    )
```

```python
import jax
import jax.numpy as jnp
from jax import lax
from jax.sharding import PartitionSpec as P

BLK = 128
NEW = 32
KEEP = 192


def rounds():
    out = []
    for axis in ("rad", "azi"):
        step = 1
        while step < lax.axis_size(axis):
            out.append((axis, step))
            step *= 2
    return out


def all_sum(x, steps):
    for axis, step in steps:
        x = x + exchange(x, axis, step)
    return x


def partner(axis, step, i):
    if axis == "azi" and step in (2, 8):
        unit = step // 2
        digit = (i // unit) % 4
        return i + (3 - digit - digit) * unit
    return i ^ step


def exchange(x, axis, step):
    count = lax.axis_size(axis)
    return lax.ppermute(x, axis, [(i, partner(axis, step, i)) for i in range(count)])


def upper_bit(axis, step):
    return (lax.axis_index(axis) // step) % 2 == 1


def halve(x, axis, step):
    half = x.shape[0] // 2
    lo, hi = x[:half], x[half:]
    bit = upper_bit(axis, step)
    return jnp.where(bit, hi, lo) + exchange(jnp.where(bit, lo, hi), axis, step)


def join(mine, other, axis, step):
    return jnp.where(
        upper_bit(axis, step),
        jnp.concatenate([other, mine], axis=0),
        jnp.concatenate([mine, other], axis=0),
    )


def pack_symmetric(g):
    return jnp.concatenate([g[:, :BLK], g[BLK:, BLK:].reshape(-1, BLK)], axis=0)


def unpack_symmetric(packed):
    tail = KEEP - BLK
    upper, lower = packed[:BLK], packed[BLK:KEEP]
    corner = packed[KEEP:].reshape(tail, tail)
    return jnp.concatenate(
        [jnp.concatenate([upper, lower.T], axis=1), jnp.concatenate([lower, corner], axis=1)], axis=0
    )


def with_halo(cells, sides, width, closed):
    for axis, dim in sides:
        count = lax.axis_size(axis)
        ends = count if closed else count - 1
        head = lax.slice_in_dim(cells, 0, width, axis=dim)
        tail = lax.slice_in_dim(cells, cells.shape[dim] - width, cells.shape[dim], axis=dim)
        cells = jnp.concatenate(
            [
                lax.ppermute(tail, axis, [(i, (i + 1) % count) for i in range(ends)]),
                cells,
                lax.ppermute(head, axis, [((i + 1) % count, i) for i in range(ends)]),
            ],
            axis=dim,
        )
    return cells


def mm(spec, a, b):
    return jnp.einsum(spec, a, b, precision=lax.Precision.HIGHEST,
                      preferred_element_type=jnp.float32)


def on_device(jacobian, new_block, kept, columns):
    rows_r = new_block.shape[0]
    rows_a = new_block.shape[1]
    elements = rows_r * rows_a
    total_rows = elements * BLK * lax.axis_size("rad") * lax.axis_size("azi")
    kept_flat = kept.reshape(elements, KEEP, BLK)
    steps = rounds()
    radial = [step for axis, step in steps if axis == "rad"]
    around = [("azi", step) for axis, step in steps if axis == "azi"]

    kept_gram = halve(pack_symmetric(mm("epi,eqi->pq", kept_flat, kept_flat)), "rad", radial[0])

    n_a, n_r = lax.axis_size("azi"), lax.axis_size("rad")
    west = lax.ppermute(new_block[:, rows_a - 1 :], "azi", [(i, (i + 1) % n_a) for i in range(n_a)])
    east = lax.ppermute(new_block[:, :1], "azi", [((i + 1) % n_a, i) for i in range(n_a)])
    kept_gram, west, east = lax.optimization_barrier((kept_gram, west, east))
    kept_gram = halve(kept_gram, "rad", radial[1])

    def row(r):
        return jnp.concatenate([west[r : r + 1], new_block[r : r + 1], east[r : r + 1]], axis=1)

    north = lax.ppermute(row(rows_r - 1), "rad", [(i, i + 1) for i in range(n_r - 1)])
    south = lax.ppermute(row(0), "rad", [(i + 1, i) for i in range(n_r - 1)])
    padded = jnp.concatenate(
        [north, jnp.concatenate([west, new_block, east], axis=1), south], axis=0
    )
    shifted = [padded[c // 3 : c // 3 + rows_r, c % 3 : c % 3 + rows_a] for c in range(9)]
    image = jnp.einsum("raij,ravj->ravi", jacobian[:, :, 0], new_block, preferred_element_type=jnp.float32)
    for k in range(1, 5):
        code = columns[:, :, k][:, :, None, None]
        pick = shifted[0]
        for c in range(1, 9):
            pick = jnp.where(code == c, shifted[c], pick)
        image = image + jnp.einsum(
            "raij,ravj->ravi", jacobian[:, :, k], pick, preferred_element_type=jnp.float32
        )
    image = image.reshape(elements, NEW, BLK)

    moments = jnp.concatenate(
        [mm("epi,evi->pv", kept_flat, image), mm("evi,ewi->vw", image, image)], axis=0
    ).reshape(-1, BLK)
    split = kept_gram.shape[0]
    ahead = 2
    joint = all_sum(
        jnp.concatenate([kept_gram, moments], axis=0),
        [("rad", step) for step in radial[ahead:]] + around,
    )
    kept_gram, moments = joint[:split], joint[split:]
    for step in reversed(radial[:ahead]):
        other = exchange(jnp.concatenate([kept_gram, moments], axis=0), "rad", step)
        moments = moments + other[kept_gram.shape[0]:]
        kept_gram = join(kept_gram, other[: kept_gram.shape[0]], "rad", step)
    kept_gram = unpack_symmetric(kept_gram)
    moments = moments.reshape(KEEP + NEW, NEW)
    first, image_gram = moments[:KEEP], moments[KEEP:]

    second = first - mm("pq,qv->pv", kept_gram, first)
    coefficients = first + second

    cross = mm("pv,pw->vw", coefficients, first)
    expanded = (
        image_gram - cross - cross.T
        + mm("pv,pw->vw", coefficients, mm("pq,qw->pw", kept_gram, coefficients))
    ) / total_rows
    eye = jnp.eye(NEW, dtype=jnp.float32)
    kept_share = jnp.sum(expanded * eye, axis=1) * 16.0 >= jnp.sum(image_gram * eye, axis=1) / total_rows

    def factor_of(gram):
        lower = jnp.linalg.cholesky(gram)
        inverse = lax.linalg.triangular_solve(lower, eye, left_side=True, lower=True)
        return lower, inverse

    def expanded_path():
        lower, inverse = factor_of(expanded)
        basis = mm("evi,wv->ewi", image, inverse) - mm(
            "epi,pw->ewi", kept_flat, mm("pv,wv->pw", coefficients, inverse)
        )
        return basis, lower

    def direct_path():
        twice = image - mm("epi,pv->evi", kept_flat, coefficients)
        lower, inverse = factor_of(all_sum(mm("evi,ewi->vw", twice, twice), steps) / total_rows)
        return mm("evi,wv->ewi", twice, inverse), lower

    basis, lower = lax.cond(jnp.all(kept_share), expanded_path, direct_path)
    basis = basis.reshape(rows_r, rows_a, NEW, BLK)
    return (basis, coefficients, lower.T)


def solution(mesh):
    return jax.shard_map(
        on_device,
        mesh=mesh,
        in_specs=(
            P("rad", "azi", None, None, None),
            P("rad", "azi", None, None),
            P("rad", "azi", None, None),
            P("rad", "azi", None),
        ),
        out_specs=(P("rad", "azi", None, None), P(), P()),
        check_vma=False,
    )
```

```python
import jax
import jax.numpy as jnp
from jax import lax
from jax.sharding import PartitionSpec as P

BLK = 128
NEW = 32
KEEP = 192


def rounds():
    out = []
    for axis in ("rad", "azi"):
        step = 1
        while step < lax.axis_size(axis):
            out.append((axis, step))
            step *= 2
    return out


def all_sum(x, steps):
    for axis, step in steps:
        x = x + exchange(x, axis, step)
    return x


def partner(axis, step, i):
    if axis == "azi" and step in (2, 8):
        unit = step // 2
        digit = (i // unit) % 4
        return i + (3 - digit - digit) * unit
    return i ^ step


def exchange(x, axis, step):
    count = lax.axis_size(axis)
    return lax.ppermute(x, axis, [(i, partner(axis, step, i)) for i in range(count)])


def upper_bit(axis, step):
    return (lax.axis_index(axis) // step) % 2 == 1


def halve(x, axis, step):
    half = x.shape[0] // 2
    lo, hi = x[:half], x[half:]
    bit = upper_bit(axis, step)
    return jnp.where(bit, hi, lo) + exchange(jnp.where(bit, lo, hi), axis, step)


def join(mine, other, axis, step):
    return jnp.where(
        upper_bit(axis, step),
        jnp.concatenate([other, mine], axis=0),
        jnp.concatenate([mine, other], axis=0),
    )


def pack_symmetric(g):
    return jnp.concatenate([g[:, :BLK], g[BLK:, BLK:].reshape(-1, BLK)], axis=0)


def unpack_symmetric(packed):
    tail = KEEP - BLK
    upper, lower = packed[:BLK], packed[BLK:KEEP]
    corner = packed[KEEP:].reshape(tail, tail)
    return jnp.concatenate(
        [jnp.concatenate([upper, lower.T], axis=1), jnp.concatenate([lower, corner], axis=1)], axis=0
    )


def with_halo(cells, sides, width, closed):
    for axis, dim in sides:
        count = lax.axis_size(axis)
        ends = count if closed else count - 1
        head = lax.slice_in_dim(cells, 0, width, axis=dim)
        tail = lax.slice_in_dim(cells, cells.shape[dim] - width, cells.shape[dim], axis=dim)
        cells = jnp.concatenate(
            [
                lax.ppermute(tail, axis, [(i, (i + 1) % count) for i in range(ends)]),
                cells,
                lax.ppermute(head, axis, [((i + 1) % count, i) for i in range(ends)]),
            ],
            axis=dim,
        )
    return cells


def mm(spec, a, b):
    return jnp.einsum(spec, a, b, precision=lax.Precision.HIGHEST,
                      preferred_element_type=jnp.float32)


def on_device(jacobian, new_block, kept, columns):
    rows_r = new_block.shape[0]
    rows_a = new_block.shape[1]
    elements = rows_r * rows_a
    total_rows = elements * BLK * lax.axis_size("rad") * lax.axis_size("azi")
    kept_flat = kept.reshape(elements, KEEP, BLK)
    steps = rounds()
    radial = [step for axis, step in steps if axis == "rad"]
    around = [("azi", step) for axis, step in steps if axis == "azi"]

    n_a, n_r = lax.axis_size("azi"), lax.axis_size("rad")
    west = lax.ppermute(new_block[:, rows_a - 1 :], "azi", [(i, (i + 1) % n_a) for i in range(n_a)])
    east = lax.ppermute(new_block[:, :1], "azi", [((i + 1) % n_a, i) for i in range(n_a)])
    kept_gram = pack_symmetric(mm("epi,eqi->pq", kept_flat, kept_flat))
    kept_gram, west, east = lax.optimization_barrier((kept_gram, west, east))
    kept_gram = halve(halve(kept_gram, "rad", radial[0]), "rad", radial[1])

    def row(r):
        return jnp.concatenate([west[r : r + 1], new_block[r : r + 1], east[r : r + 1]], axis=1)

    north = lax.ppermute(row(rows_r - 1), "rad", [(i, i + 1) for i in range(n_r - 1)])
    south = lax.ppermute(row(0), "rad", [(i + 1, i) for i in range(n_r - 1)])
    padded = jnp.concatenate(
        [north, jnp.concatenate([west, new_block, east], axis=1), south], axis=0
    )
    kept_gram, padded = lax.optimization_barrier((kept_gram, padded))
    shifted = [padded[c // 3 : c // 3 + rows_r, c % 3 : c % 3 + rows_a] for c in range(9)]
    image = jnp.einsum("raij,ravj->ravi", jacobian[:, :, 0], new_block, preferred_element_type=jnp.float32)
    for k in range(1, 5):
        code = columns[:, :, k][:, :, None, None]
        pick = shifted[0]
        for c in range(1, 9):
            pick = jnp.where(code == c, shifted[c], pick)
        image = image + jnp.einsum(
            "raij,ravj->ravi", jacobian[:, :, k], pick, preferred_element_type=jnp.float32
        )
    image = image.reshape(elements, NEW, BLK)

    moments = jnp.concatenate(
        [mm("epi,evi->pv", kept_flat, image), mm("evi,ewi->vw", image, image)], axis=0
    ).reshape(-1, BLK)
    split = kept_gram.shape[0]
    ahead = 2
    joint = all_sum(
        jnp.concatenate([kept_gram, moments], axis=0),
        [("rad", step) for step in radial[ahead:]] + around,
    )
    kept_gram, moments = joint[:split], joint[split:]
    for step in reversed(radial[:ahead]):
        other = exchange(jnp.concatenate([kept_gram, moments], axis=0), "rad", step)
        moments = moments + other[kept_gram.shape[0]:]
        kept_gram = join(kept_gram, other[: kept_gram.shape[0]], "rad", step)
    kept_gram = unpack_symmetric(kept_gram)
    moments = moments.reshape(KEEP + NEW, NEW)
    first, image_gram = moments[:KEEP], moments[KEEP:]

    second = first - mm("pq,qv->pv", kept_gram, first)
    coefficients = first + second

    cross = mm("pv,pw->vw", coefficients, first)
    expanded = (
        image_gram - cross - cross.T
        + mm("pv,pw->vw", coefficients, mm("pq,qw->pw", kept_gram, coefficients))
    ) / total_rows
    eye = jnp.eye(NEW, dtype=jnp.float32)
    kept_share = jnp.sum(expanded * eye, axis=1) * 16.0 >= jnp.sum(image_gram * eye, axis=1) / total_rows

    def factor_of(gram):
        lower = jnp.linalg.cholesky(gram)
        inverse = lax.linalg.triangular_solve(lower, eye, left_side=True, lower=True)
        return lower, inverse

    def expanded_path():
        lower, inverse = factor_of(expanded)
        basis = mm("evi,wv->ewi", image, inverse) - mm(
            "epi,pw->ewi", kept_flat, mm("pv,wv->pw", coefficients, inverse)
        )
        return basis, lower

    def direct_path():
        twice = image - mm("epi,pv->evi", kept_flat, coefficients)
        lower, inverse = factor_of(all_sum(mm("evi,ewi->vw", twice, twice), steps) / total_rows)
        return mm("evi,wv->ewi", twice, inverse), lower

    basis, lower = lax.cond(jnp.all(kept_share), expanded_path, direct_path)
    basis = basis.reshape(rows_r, rows_a, NEW, BLK)
    return (basis, coefficients, lower.T)


def solution(mesh):
    return jax.shard_map(
        on_device,
        mesh=mesh,
        in_specs=(
            P("rad", "azi", None, None, None),
            P("rad", "azi", None, None),
            P("rad", "azi", None, None),
            P("rad", "azi", None),
        ),
        out_specs=(P("rad", "azi", None, None), P(), P()),
        check_vma=False,
    )
```

```python
import jax
import jax.numpy as jnp
from jax import lax
from jax.sharding import PartitionSpec as P

BLK = 128
NEW = 32
KEEP = 192


def rounds():
    out = []
    for axis in ("rad", "azi"):
        step = 1
        while step < lax.axis_size(axis):
            out.append((axis, step))
            step *= 2
    return out


def all_sum(x, steps):
    for axis, step in steps:
        count = lax.axis_size(axis)
        x = x + lax.ppermute(x, axis, [(i, i ^ step) for i in range(count)])
    return x


def exchange(x, axis, step):
    count = lax.axis_size(axis)
    return lax.ppermute(x, axis, [(i, i ^ step) for i in range(count)])


def upper_bit(axis, step):
    return (lax.axis_index(axis) // step) % 2 == 1


def halve(x, axis, step):
    half = x.shape[0] // 2
    lo, hi = x[:half], x[half:]
    bit = upper_bit(axis, step)
    return jnp.where(bit, hi, lo) + exchange(jnp.where(bit, lo, hi), axis, step)


def join(mine, other, axis, step):
    return jnp.where(
        upper_bit(axis, step),
        jnp.concatenate([other, mine], axis=0),
        jnp.concatenate([mine, other], axis=0),
    )


def pack_symmetric(g):
    return jnp.concatenate([g[:, :BLK], g[BLK:, BLK:].reshape(-1, BLK)], axis=0)


def unpack_symmetric(packed):
    tail = KEEP - BLK
    upper, lower = packed[:BLK], packed[BLK:KEEP]
    corner = packed[KEEP:].reshape(tail, tail)
    return jnp.concatenate(
        [jnp.concatenate([upper, lower.T], axis=1), jnp.concatenate([lower, corner], axis=1)], axis=0
    )


def with_halo(cells, sides, width, closed):
    for axis, dim in sides:
        count = lax.axis_size(axis)
        ends = count if closed else count - 1
        head = lax.slice_in_dim(cells, 0, width, axis=dim)
        tail = lax.slice_in_dim(cells, cells.shape[dim] - width, cells.shape[dim], axis=dim)
        cells = jnp.concatenate(
            [
                lax.ppermute(tail, axis, [(i, (i + 1) % count) for i in range(ends)]),
                cells,
                lax.ppermute(head, axis, [((i + 1) % count, i) for i in range(ends)]),
            ],
            axis=dim,
        )
    return cells


def mm(spec, a, b):
    return jnp.einsum(spec, a, b, precision=lax.Precision.HIGHEST,
                      preferred_element_type=jnp.float32)


def on_device(jacobian, new_block, kept, columns):
    rows_r = new_block.shape[0]
    rows_a = new_block.shape[1]
    elements = rows_r * rows_a
    total_rows = elements * BLK * lax.axis_size("rad") * lax.axis_size("azi")
    kept_flat = kept.reshape(elements, KEEP, BLK)
    steps = rounds()
    radial = [step for axis, step in steps if axis == "rad"]
    around = [("azi", step) for axis, step in steps if axis == "azi"]

    kept_gram = halve(pack_symmetric(mm("epi,eqi->pq", kept_flat, kept_flat)), "rad", radial[0])

    n_a, n_r = lax.axis_size("azi"), lax.axis_size("rad")
    west = lax.ppermute(new_block[:, rows_a - 1 :], "azi", [(i, (i + 1) % n_a) for i in range(n_a)])
    east = lax.ppermute(new_block[:, :1], "azi", [((i + 1) % n_a, i) for i in range(n_a)])
    kept_gram, west, east = lax.optimization_barrier((kept_gram, west, east))
    kept_gram = halve(kept_gram, "rad", radial[1])

    def row(r):
        return jnp.concatenate([west[r : r + 1], new_block[r : r + 1], east[r : r + 1]], axis=1)

    north = lax.ppermute(row(rows_r - 1), "rad", [(i, i + 1) for i in range(n_r - 1)])
    south = lax.ppermute(row(0), "rad", [(i + 1, i) for i in range(n_r - 1)])
    padded = jnp.concatenate(
        [north, jnp.concatenate([west, new_block, east], axis=1), south], axis=0
    )
    shifted = [padded[c // 3 : c // 3 + rows_r, c % 3 : c % 3 + rows_a] for c in range(9)]
    slots = [new_block]
    for k in range(1, 5):
        code = columns[:, :, k][:, :, None, None]
        pick = shifted[0]
        for c in range(1, 9):
            pick = jnp.where(code == c, shifted[c], pick)
        slots.append(pick)
    picked = jnp.stack(slots, axis=2)
    image = jnp.einsum("rakij,rakvj->ravi", jacobian, picked, preferred_element_type=jnp.float32)
    image = image.reshape(elements, NEW, BLK)

    moments = jnp.concatenate(
        [mm("epi,evi->pv", kept_flat, image), mm("evi,ewi->vw", image, image)], axis=0
    ).reshape(-1, BLK)
    split = kept_gram.shape[0]
    ahead = 2
    joint = all_sum(
        jnp.concatenate([kept_gram, moments], axis=0),
        [("rad", step) for step in radial[ahead:]] + around,
    )
    kept_gram, moments = joint[:split], joint[split:]
    for step in reversed(radial[:ahead]):
        other = exchange(jnp.concatenate([kept_gram, moments], axis=0), "rad", step)
        moments = moments + other[kept_gram.shape[0]:]
        kept_gram = join(kept_gram, other[: kept_gram.shape[0]], "rad", step)
    kept_gram = unpack_symmetric(kept_gram)
    moments = moments.reshape(KEEP + NEW, NEW)
    first, image_gram = moments[:KEEP], moments[KEEP:]

    second = first - mm("pq,qv->pv", kept_gram, first)
    coefficients = first + second

    cross = mm("pv,pw->vw", coefficients, first)
    expanded = (
        image_gram - cross - cross.T
        + mm("pv,pw->vw", coefficients, mm("pq,qw->pw", kept_gram, coefficients))
    ) / total_rows
    eye = jnp.eye(NEW, dtype=jnp.float32)
    kept_share = jnp.sum(expanded * eye, axis=1) * 16.0 >= jnp.sum(image_gram * eye, axis=1) / total_rows

    def factor_of(gram):
        lower = jnp.linalg.cholesky(gram)
        inverse = lax.linalg.triangular_solve(lower, eye, left_side=True, lower=True)
        return lower, inverse

    def expanded_path():
        lower, inverse = factor_of(expanded)
        fast = lax.Precision.HIGH
        basis = jnp.einsum(
            "evi,wv->ewi", image, inverse, precision=fast, preferred_element_type=jnp.float32
        ) - jnp.einsum(
            "epi,pw->ewi", kept_flat, mm("pv,wv->pw", coefficients, inverse),
            precision=fast, preferred_element_type=jnp.float32,
        )
        return basis, lower

    def direct_path():
        twice = image - mm("epi,pv->evi", kept_flat, coefficients)
        lower, inverse = factor_of(all_sum(mm("evi,ewi->vw", twice, twice), steps) / total_rows)
        return mm("evi,wv->ewi", twice, inverse), lower

    basis, lower = lax.cond(jnp.all(kept_share), expanded_path, direct_path)
    basis = basis.reshape(rows_r, rows_a, NEW, BLK)
    return (basis, coefficients, lower.T)


def solution(mesh):
    return jax.shard_map(
        on_device,
        mesh=mesh,
        in_specs=(
            P("rad", "azi", None, None, None),
            P("rad", "azi", None, None),
            P("rad", "azi", None, None),
            P("rad", "azi", None),
        ),
        out_specs=(P("rad", "azi", None, None), P(), P()),
        check_vma=False,
    )
```

```python
import jax
import jax.numpy as jnp
from jax import lax
from jax.sharding import PartitionSpec as P

BLK = 128
NEW = 32
KEEP = 192


def rounds():
    out = []
    for axis in ("rad", "azi"):
        step = 1
        while step < lax.axis_size(axis):
            out.append((axis, step))
            step *= 2
    return out


def all_sum(x, steps):
    for axis, step in steps:
        count = lax.axis_size(axis)
        x = x + lax.ppermute(x, axis, [(i, i ^ step) for i in range(count)])
    return x


def exchange(x, axis, step):
    count = lax.axis_size(axis)
    return lax.ppermute(x, axis, [(i, i ^ step) for i in range(count)])


def upper_bit(axis, step):
    return (lax.axis_index(axis) // step) % 2 == 1


def halve(x, axis, step):
    half = x.shape[0] // 2
    lo, hi = x[:half], x[half:]
    bit = upper_bit(axis, step)
    return jnp.where(bit, hi, lo) + exchange(jnp.where(bit, lo, hi), axis, step)


def join(mine, other, axis, step):
    return jnp.where(
        upper_bit(axis, step),
        jnp.concatenate([other, mine], axis=0),
        jnp.concatenate([mine, other], axis=0),
    )


def pack_symmetric(g):
    return jnp.concatenate([g[:, :BLK], g[BLK:, BLK:].reshape(-1, BLK)], axis=0)


def unpack_symmetric(packed):
    tail = KEEP - BLK
    upper, lower = packed[:BLK], packed[BLK:KEEP]
    corner = packed[KEEP:].reshape(tail, tail)
    return jnp.concatenate(
        [jnp.concatenate([upper, lower.T], axis=1), jnp.concatenate([lower, corner], axis=1)], axis=0
    )


def with_halo(cells, sides, width, closed):
    for axis, dim in sides:
        count = lax.axis_size(axis)
        ends = count if closed else count - 1
        head = lax.slice_in_dim(cells, 0, width, axis=dim)
        tail = lax.slice_in_dim(cells, cells.shape[dim] - width, cells.shape[dim], axis=dim)
        cells = jnp.concatenate(
            [
                lax.ppermute(tail, axis, [(i, (i + 1) % count) for i in range(ends)]),
                cells,
                lax.ppermute(head, axis, [((i + 1) % count, i) for i in range(ends)]),
            ],
            axis=dim,
        )
    return cells


def mm(spec, a, b):
    return jnp.einsum(spec, a, b, precision=lax.Precision.HIGHEST,
                      preferred_element_type=jnp.float32)


def on_device(jacobian, new_block, kept, columns):
    rows_r = new_block.shape[0]
    rows_a = new_block.shape[1]
    elements = rows_r * rows_a
    total_rows = elements * BLK * lax.axis_size("rad") * lax.axis_size("azi")
    kept_flat = kept.reshape(elements, KEEP, BLK)
    steps = rounds()
    radial = [step for axis, step in steps if axis == "rad"]
    around = [("azi", step) for axis, step in steps if axis == "azi"]

    kept_gram = halve(pack_symmetric(mm("epi,eqi->pq", kept_flat, kept_flat)), "rad", radial[0])

    n_a, n_r = lax.axis_size("azi"), lax.axis_size("rad")
    west = lax.ppermute(new_block[:, rows_a - 1 :], "azi", [(i, (i + 1) % n_a) for i in range(n_a)])
    east = lax.ppermute(new_block[:, :1], "azi", [((i + 1) % n_a, i) for i in range(n_a)])
    kept_gram, west, east = lax.optimization_barrier((kept_gram, west, east))
    kept_gram = halve(kept_gram, "rad", radial[1])

    def row(r):
        return jnp.concatenate([west[r : r + 1], new_block[r : r + 1], east[r : r + 1]], axis=1)

    north = lax.ppermute(row(rows_r - 1), "rad", [(i, i + 1) for i in range(n_r - 1)])
    south = lax.ppermute(row(0), "rad", [(i + 1, i) for i in range(n_r - 1)])
    padded = jnp.concatenate(
        [north, jnp.concatenate([west, new_block, east], axis=1), south], axis=0
    )
    shifted = [padded[c // 3 : c // 3 + rows_r, c % 3 : c % 3 + rows_a] for c in range(9)]
    slots = [new_block]
    for k in range(1, 5):
        code = columns[:, :, k][:, :, None, None]
        pick = shifted[0]
        for c in range(1, 9):
            pick = jnp.where(code == c, shifted[c], pick)
        slots.append(pick)
    picked = jnp.stack(slots, axis=2)
    image = jnp.einsum("rakij,rakvj->ravi", jacobian, picked, preferred_element_type=jnp.float32)
    image = image.reshape(elements, NEW, BLK)

    moments = jnp.concatenate(
        [mm("epi,evi->pv", kept_flat, image), mm("evi,ewi->vw", image, image)], axis=0
    ).reshape(-1, BLK)
    split = kept_gram.shape[0]
    ahead = 2
    joint = all_sum(
        jnp.concatenate([kept_gram, moments], axis=0),
        [("rad", step) for step in radial[ahead:]] + around,
    )
    kept_gram, moments = joint[:split], joint[split:]
    for step in reversed(radial[:ahead]):
        other = exchange(jnp.concatenate([kept_gram, moments], axis=0), "rad", step)
        moments = moments + other[kept_gram.shape[0]:]
        kept_gram = join(kept_gram, other[: kept_gram.shape[0]], "rad", step)
    kept_gram = unpack_symmetric(kept_gram)
    moments = moments.reshape(KEEP + NEW, NEW)
    first, image_gram = moments[:KEEP], moments[KEEP:]

    second = first - mm("pq,qv->pv", kept_gram, first)
    coefficients = first + second

    cross = mm("pv,pw->vw", coefficients, first)
    expanded = (
        image_gram - cross - cross.T
        + mm("pv,pw->vw", coefficients, mm("pq,qw->pw", kept_gram, coefficients))
    ) / total_rows
    eye = jnp.eye(NEW, dtype=jnp.float32)
    kept_share = jnp.min(jnp.sum(expanded * 16.0 - image_gram / total_rows, axis=1, where=eye > 0)) >= 0.0

    def factor_of(gram):
        lower = jnp.linalg.cholesky(gram)
        inverse = lax.linalg.triangular_solve(lower, eye, left_side=True, lower=True)
        return lower, inverse

    def expanded_path():
        lower, inverse = factor_of(expanded)
        fast = lax.Precision.HIGH
        basis = jnp.einsum(
            "evi,wv->ewi", image, inverse, precision=fast, preferred_element_type=jnp.float32
        ) - jnp.einsum(
            "epi,pw->ewi", kept_flat, mm("pv,wv->pw", coefficients, inverse),
            precision=fast, preferred_element_type=jnp.float32,
        )
        return basis, lower

    def direct_path():
        twice = image - mm("epi,pv->evi", kept_flat, coefficients)
        lower, inverse = factor_of(all_sum(mm("evi,ewi->vw", twice, twice), steps) / total_rows)
        return mm("evi,wv->ewi", twice, inverse), lower

    basis, lower = lax.cond(kept_share, expanded_path, direct_path)
    basis = basis.reshape(rows_r, rows_a, NEW, BLK)
    return (basis, coefficients, lower.T)


def solution(mesh):
    return jax.shard_map(
        on_device,
        mesh=mesh,
        in_specs=(
            P("rad", "azi", None, None, None),
            P("rad", "azi", None, None),
            P("rad", "azi", None, None),
            P("rad", "azi", None),
        ),
        out_specs=(P("rad", "azi", None, None), P(), P()),
        check_vma=False,
    )
```

```python
import jax
import jax.numpy as jnp
from jax import lax
from jax.sharding import PartitionSpec as P

BLK = 128
NEW = 32
KEEP = 192


def rounds():
    out = []
    for axis in ("rad", "azi"):
        step = 1
        while step < lax.axis_size(axis):
            out.append((axis, step))
            step *= 2
    return out


def all_sum(x, steps):
    for axis, step in steps:
        x = x + exchange(x, axis, step)
    return x


def partner(axis, step, i):
    if axis == "azi" and step in (2, 8):
        unit = step // 2
        digit = (i // unit) % 4
        return i + (3 - digit - digit) * unit
    return i ^ step


def exchange(x, axis, step):
    count = lax.axis_size(axis)
    return lax.ppermute(x, axis, [(i, partner(axis, step, i)) for i in range(count)])


def upper_bit(axis, step):
    return (lax.axis_index(axis) // step) % 2 == 1


def halve(x, axis, step):
    half = x.shape[0] // 2
    lo, hi = x[:half], x[half:]
    bit = upper_bit(axis, step)
    return jnp.where(bit, hi, lo) + exchange(jnp.where(bit, lo, hi), axis, step)


def join(mine, other, axis, step):
    return jnp.where(
        upper_bit(axis, step),
        jnp.concatenate([other, mine], axis=0),
        jnp.concatenate([mine, other], axis=0),
    )


def pack_symmetric(g):
    return jnp.concatenate([g[:, :BLK], g[BLK:, BLK:].reshape(-1, BLK)], axis=0)


def unpack_symmetric(packed):
    tail = KEEP - BLK
    upper, lower = packed[:BLK], packed[BLK:KEEP]
    corner = packed[KEEP:].reshape(tail, tail)
    return jnp.concatenate(
        [jnp.concatenate([upper, lower.T], axis=1), jnp.concatenate([lower, corner], axis=1)], axis=0
    )


def with_halo(cells, sides, width, closed):
    for axis, dim in sides:
        count = lax.axis_size(axis)
        ends = count if closed else count - 1
        head = lax.slice_in_dim(cells, 0, width, axis=dim)
        tail = lax.slice_in_dim(cells, cells.shape[dim] - width, cells.shape[dim], axis=dim)
        cells = jnp.concatenate(
            [
                lax.ppermute(tail, axis, [(i, (i + 1) % count) for i in range(ends)]),
                cells,
                lax.ppermute(head, axis, [((i + 1) % count, i) for i in range(ends)]),
            ],
            axis=dim,
        )
    return cells


def mm(spec, a, b):
    return jnp.einsum(spec, a, b, precision=lax.Precision.HIGHEST,
                      preferred_element_type=jnp.float32)


def on_device(jacobian, new_block, kept, columns):
    rows_r = new_block.shape[0]
    rows_a = new_block.shape[1]
    elements = rows_r * rows_a
    total_rows = elements * BLK * lax.axis_size("rad") * lax.axis_size("azi")
    kept_flat = kept.reshape(elements, KEEP, BLK)
    steps = rounds()
    radial = [step for axis, step in steps if axis == "rad"]
    around = [("azi", step) for axis, step in steps if axis == "azi"]

    kept_gram = halve(pack_symmetric(mm("epi,eqi->pq", kept_flat, kept_flat)), "rad", radial[0])

    n_a, n_r = lax.axis_size("azi"), lax.axis_size("rad")
    west = lax.ppermute(new_block[:, rows_a - 1 :], "azi", [(i, (i + 1) % n_a) for i in range(n_a)])
    east = lax.ppermute(new_block[:, :1], "azi", [((i + 1) % n_a, i) for i in range(n_a)])
    kept_gram, west, east = lax.optimization_barrier((kept_gram, west, east))
    kept_gram = halve(kept_gram, "rad", radial[1])

    def row(r):
        return jnp.concatenate([west[r : r + 1], new_block[r : r + 1], east[r : r + 1]], axis=1)

    north = lax.ppermute(row(rows_r - 1), "rad", [(i, i + 1) for i in range(n_r - 1)])
    south = lax.ppermute(row(0), "rad", [(i + 1, i) for i in range(n_r - 1)])
    padded = jnp.concatenate(
        [north, jnp.concatenate([west, new_block, east], axis=1), south], axis=0
    )
    shifted = [padded[c // 3 : c // 3 + rows_r, c % 3 : c % 3 + rows_a] for c in range(9)]
    slots = [new_block]
    for k in range(1, 5):
        code = columns[:, :, k][:, :, None, None]
        pick = shifted[0]
        for c in range(1, 9):
            pick = jnp.where(code == c, shifted[c], pick)
        slots.append(pick)
    picked = jnp.stack(slots, axis=2)
    image = jnp.einsum("rakij,rakvj->ravi", jacobian, picked, preferred_element_type=jnp.float32)
    image = image.reshape(elements, NEW, BLK)

    moments = jnp.concatenate(
        [mm("epi,evi->pv", kept_flat, image), mm("evi,ewi->vw", image, image)], axis=0
    ).reshape(-1, BLK)
    split = kept_gram.shape[0]
    ahead = 2
    joint = all_sum(
        jnp.concatenate([kept_gram, moments], axis=0),
        [("rad", step) for step in radial[ahead:]] + around,
    )
    kept_gram, moments = joint[:split], joint[split:]
    for step in reversed(radial[:ahead]):
        other = exchange(jnp.concatenate([kept_gram, moments], axis=0), "rad", step)
        moments = moments + other[kept_gram.shape[0]:]
        kept_gram = join(kept_gram, other[: kept_gram.shape[0]], "rad", step)
    kept_gram = unpack_symmetric(kept_gram)
    moments = moments.reshape(KEEP + NEW, NEW)
    first, image_gram = moments[:KEEP], moments[KEEP:]

    second = first - mm("pq,qv->pv", kept_gram, first)
    coefficients = first + second

    cross = mm("pv,pw->vw", coefficients, first)
    expanded = (
        image_gram - cross - cross.T
        + mm("pv,pw->vw", coefficients, mm("pq,qw->pw", kept_gram, coefficients))
    ) / total_rows
    eye = jnp.eye(NEW, dtype=jnp.float32)
    kept_share = jnp.sum(expanded * eye, axis=1) * 16.0 >= jnp.sum(image_gram * eye, axis=1) / total_rows

    def factor_of(gram):
        lower = jnp.linalg.cholesky(gram)
        inverse = lax.linalg.triangular_solve(lower, eye, left_side=True, lower=True)
        return lower, inverse

    def expanded_path():
        lower, inverse = factor_of(expanded)
        fast = lax.Precision.HIGH
        basis = jnp.einsum(
            "evi,wv->ewi", image, inverse, precision=fast, preferred_element_type=jnp.float32
        ) - jnp.einsum(
            "epi,pw->ewi", kept_flat, mm("pv,wv->pw", coefficients, inverse),
            precision=fast, preferred_element_type=jnp.float32,
        )
        return basis, lower

    def direct_path():
        twice = image - mm("epi,pv->evi", kept_flat, coefficients)
        lower, inverse = factor_of(all_sum(mm("evi,ewi->vw", twice, twice), steps) / total_rows)
        return mm("evi,wv->ewi", twice, inverse), lower

    basis, lower = lax.cond(jnp.all(kept_share), expanded_path, direct_path)
    basis = basis.reshape(rows_r, rows_a, NEW, BLK)
    return (basis, coefficients, lower.T)


def solution(mesh):
    return jax.shard_map(
        on_device,
        mesh=mesh,
        in_specs=(
            P("rad", "azi", None, None, None),
            P("rad", "azi", None, None),
            P("rad", "azi", None, None),
            P("rad", "azi", None),
        ),
        out_specs=(P("rad", "azi", None, None), P(), P()),
        check_vma=False,
    )
```

```python
import jax
import jax.numpy as jnp
from jax import lax
from jax.sharding import PartitionSpec as P

BLK = 128
NEW = 32
KEEP = 192


def rounds():
    out = []
    for axis in ("rad", "azi"):
        step = 1
        while step < lax.axis_size(axis):
            out.append((axis, step))
            step *= 2
    return out


def all_sum(x, steps):
    for axis, step in steps:
        count = lax.axis_size(axis)
        x = x + lax.ppermute(x, axis, [(i, i ^ step) for i in range(count)])
    return x


def exchange(x, axis, step):
    count = lax.axis_size(axis)
    return lax.ppermute(x, axis, [(i, i ^ step) for i in range(count)])


def upper_bit(axis, step):
    return (lax.axis_index(axis) // step) % 2 == 1


def halve(x, axis, step):
    half = x.shape[0] // 2
    lo, hi = x[:half], x[half:]
    bit = upper_bit(axis, step)
    return jnp.where(bit, hi, lo) + exchange(jnp.where(bit, lo, hi), axis, step)


def join(mine, other, axis, step):
    return jnp.where(
        upper_bit(axis, step),
        jnp.concatenate([other, mine], axis=0),
        jnp.concatenate([mine, other], axis=0),
    )


def pack_symmetric(g):
    return jnp.concatenate([g[:, :BLK], g[BLK:, BLK:].reshape(-1, BLK)], axis=0)


def unpack_symmetric(packed):
    tail = KEEP - BLK
    upper, lower = packed[:BLK], packed[BLK:KEEP]
    corner = packed[KEEP:].reshape(tail, tail)
    return jnp.concatenate(
        [jnp.concatenate([upper, lower.T], axis=1), jnp.concatenate([lower, corner], axis=1)], axis=0
    )


def with_halo(cells, sides, width, closed):
    for axis, dim in sides:
        count = lax.axis_size(axis)
        ends = count if closed else count - 1
        head = lax.slice_in_dim(cells, 0, width, axis=dim)
        tail = lax.slice_in_dim(cells, cells.shape[dim] - width, cells.shape[dim], axis=dim)
        cells = jnp.concatenate(
            [
                lax.ppermute(tail, axis, [(i, (i + 1) % count) for i in range(ends)]),
                cells,
                lax.ppermute(head, axis, [((i + 1) % count, i) for i in range(ends)]),
            ],
            axis=dim,
        )
    return cells


def mm(spec, a, b):
    return jnp.einsum(spec, a, b, precision=lax.Precision.HIGHEST,
                      preferred_element_type=jnp.float32)


def on_device(jacobian, new_block, kept, columns):
    rows_r = new_block.shape[0]
    rows_a = new_block.shape[1]
    elements = rows_r * rows_a
    total_rows = elements * BLK * lax.axis_size("rad") * lax.axis_size("azi")
    kept_flat = kept.reshape(elements, KEEP, BLK)
    steps = rounds()
    radial = [step for axis, step in steps if axis == "rad"]
    around = [("azi", step) for axis, step in steps if axis == "azi"]

    kept_gram = halve(pack_symmetric(jnp.einsum(
        "epi,eqi->pq", kept_flat, kept_flat, precision=lax.Precision.HIGH,
        preferred_element_type=jnp.float32)), "rad", radial[0])

    n_a, n_r = lax.axis_size("azi"), lax.axis_size("rad")
    west = lax.ppermute(new_block[:, rows_a - 1 :], "azi", [(i, (i + 1) % n_a) for i in range(n_a)])
    east = lax.ppermute(new_block[:, :1], "azi", [((i + 1) % n_a, i) for i in range(n_a)])
    kept_gram, west, east = lax.optimization_barrier((kept_gram, west, east))
    kept_gram = halve(kept_gram, "rad", radial[1])

    def row(r):
        return jnp.concatenate([west[r : r + 1], new_block[r : r + 1], east[r : r + 1]], axis=1)

    north = lax.ppermute(row(rows_r - 1), "rad", [(i, i + 1) for i in range(n_r - 1)])
    south = lax.ppermute(row(0), "rad", [(i + 1, i) for i in range(n_r - 1)])
    padded = jnp.concatenate(
        [north, jnp.concatenate([west, new_block, east], axis=1), south], axis=0
    )
    shifted = [padded[c // 3 : c // 3 + rows_r, c % 3 : c % 3 + rows_a] for c in range(9)]
    image = jnp.einsum("raij,ravj->ravi", jacobian[:, :, 0], new_block, preferred_element_type=jnp.float32)
    for k in range(1, 5):
        code = columns[:, :, k][:, :, None, None]
        pick = shifted[0]
        for c in range(1, 9):
            pick = jnp.where(code == c, shifted[c], pick)
        image = image + jnp.einsum(
            "raij,ravj->ravi", jacobian[:, :, k], pick, preferred_element_type=jnp.float32
        )
    image = image.reshape(elements, NEW, BLK)

    moments = jnp.concatenate(
        [mm("epi,evi->pv", kept_flat, image), mm("evi,ewi->vw", image, image)], axis=0
    ).reshape(-1, BLK)
    split = kept_gram.shape[0]
    ahead = 2
    joint = all_sum(
        jnp.concatenate([kept_gram, moments], axis=0),
        [("rad", step) for step in radial[ahead:]] + around,
    )
    kept_gram, moments = joint[:split], joint[split:]
    for step in reversed(radial[:ahead]):
        other = exchange(jnp.concatenate([kept_gram, moments], axis=0), "rad", step)
        moments = moments + other[kept_gram.shape[0]:]
        kept_gram = join(kept_gram, other[: kept_gram.shape[0]], "rad", step)
    kept_gram = unpack_symmetric(kept_gram)
    moments = moments.reshape(KEEP + NEW, NEW)
    first, image_gram = moments[:KEEP], moments[KEEP:]

    second = first - mm("pq,qv->pv", kept_gram, first)
    coefficients = first + second

    cross = mm("pv,pw->vw", coefficients, first)
    expanded = (
        image_gram - cross - cross.T
        + mm("pv,pw->vw", coefficients, mm("pq,qw->pw", kept_gram, coefficients))
    ) / total_rows
    eye = jnp.eye(NEW, dtype=jnp.float32)
    kept_share = jnp.sum(expanded * eye, axis=1) * 16.0 >= jnp.sum(image_gram * eye, axis=1) / total_rows

    def factor_of(gram):
        lower = jnp.linalg.cholesky(gram)
        inverse = lax.linalg.triangular_solve(lower, eye, left_side=True, lower=True)
        return lower, inverse

    def expanded_path():
        lower, inverse = factor_of(expanded)
        fast = lax.Precision.HIGH
        basis = jnp.einsum(
            "evi,wv->ewi", image, inverse, precision=fast, preferred_element_type=jnp.float32
        ) - jnp.einsum(
            "epi,pw->ewi", kept_flat, mm("pv,wv->pw", coefficients, inverse),
            precision=fast, preferred_element_type=jnp.float32,
        )
        return basis, lower

    def direct_path():
        twice = image - mm("epi,pv->evi", kept_flat, coefficients)
        lower, inverse = factor_of(all_sum(mm("evi,ewi->vw", twice, twice), steps) / total_rows)
        return mm("evi,wv->ewi", twice, inverse), lower

    basis, lower = lax.cond(jnp.all(kept_share), expanded_path, direct_path)
    basis = basis.reshape(rows_r, rows_a, NEW, BLK)
    return (basis, coefficients, lower.T)


def solution(mesh):
    return jax.shard_map(
        on_device,
        mesh=mesh,
        in_specs=(
            P("rad", "azi", None, None, None),
            P("rad", "azi", None, None),
            P("rad", "azi", None, None),
            P("rad", "azi", None),
        ),
        out_specs=(P("rad", "azi", None, None), P(), P()),
        check_vma=False,
    )
```

```python
import jax
import jax.numpy as jnp
from jax import lax
from jax.sharding import PartitionSpec as P

BLK = 128
NEW = 32
KEEP = 192


def rounds():
    out = []
    for axis in ("rad", "azi"):
        step = 1
        while step < lax.axis_size(axis):
            out.append((axis, step))
            step *= 2
    return out


def all_sum(x, steps):
    for axis, step in steps:
        count = lax.axis_size(axis)
        x = x + lax.ppermute(x, axis, [(i, i ^ step) for i in range(count)])
    return x


def exchange(x, axis, step):
    count = lax.axis_size(axis)
    return lax.ppermute(x, axis, [(i, i ^ step) for i in range(count)])


def upper_bit(axis, step):
    return (lax.axis_index(axis) // step) % 2 == 1


def halve(x, axis, step):
    half = x.shape[0] // 2
    lo, hi = x[:half], x[half:]
    bit = upper_bit(axis, step)
    return jnp.where(bit, hi, lo) + exchange(jnp.where(bit, lo, hi), axis, step)


def join(mine, other, axis, step):
    return jnp.where(
        upper_bit(axis, step),
        jnp.concatenate([other, mine], axis=0),
        jnp.concatenate([mine, other], axis=0),
    )


def pack_symmetric(g):
    return jnp.concatenate([g[:, :BLK], g[BLK:, BLK:].reshape(-1, BLK)], axis=0)


def unpack_symmetric(packed):
    tail = KEEP - BLK
    upper, lower = packed[:BLK], packed[BLK:KEEP]
    corner = packed[KEEP:].reshape(tail, tail)
    return jnp.concatenate(
        [jnp.concatenate([upper, lower.T], axis=1), jnp.concatenate([lower, corner], axis=1)], axis=0
    )


def with_halo(cells, sides, width, closed):
    for axis, dim in sides:
        count = lax.axis_size(axis)
        ends = count if closed else count - 1
        head = lax.slice_in_dim(cells, 0, width, axis=dim)
        tail = lax.slice_in_dim(cells, cells.shape[dim] - width, cells.shape[dim], axis=dim)
        cells = jnp.concatenate(
            [
                lax.ppermute(tail, axis, [(i, (i + 1) % count) for i in range(ends)]),
                cells,
                lax.ppermute(head, axis, [((i + 1) % count, i) for i in range(ends)]),
            ],
            axis=dim,
        )
    return cells


def mm(spec, a, b):
    return jnp.einsum(spec, a, b, precision=lax.Precision.HIGHEST,
                      preferred_element_type=jnp.float32)


def on_device(jacobian, new_block, kept, columns):
    rows_r = new_block.shape[0]
    rows_a = new_block.shape[1]
    elements = rows_r * rows_a
    total_rows = elements * BLK * lax.axis_size("rad") * lax.axis_size("azi")
    kept_flat = kept.reshape(elements, KEEP, BLK)
    steps = rounds()
    radial = [step for axis, step in steps if axis == "rad"]
    around = [("azi", step) for axis, step in steps if axis == "azi"]

    kept_gram = halve(pack_symmetric(mm("epi,eqi->pq", kept_flat, kept_flat)), "rad", radial[0])

    n_a, n_r = lax.axis_size("azi"), lax.axis_size("rad")
    west = lax.ppermute(new_block[:, rows_a - 1 :], "azi", [(i, (i + 1) % n_a) for i in range(n_a)])
    east = lax.ppermute(new_block[:, :1], "azi", [((i + 1) % n_a, i) for i in range(n_a)])
    kept_gram, west, east = lax.optimization_barrier((kept_gram, west, east))
    kept_gram = halve(kept_gram, "rad", radial[1])

    def row(r):
        return jnp.concatenate([west[r : r + 1], new_block[r : r + 1], east[r : r + 1]], axis=1)

    north = lax.ppermute(row(rows_r - 1), "rad", [(i, i + 1) for i in range(n_r - 1)])
    south = lax.ppermute(row(0), "rad", [(i + 1, i) for i in range(n_r - 1)])
    padded = jnp.concatenate(
        [north, jnp.concatenate([west, new_block, east], axis=1), south], axis=0
    )
    shifted = [padded[c // 3 : c // 3 + rows_r, c % 3 : c % 3 + rows_a] for c in range(9)]
    slots = [new_block]
    for k in range(1, 5):
        code = columns[:, :, k][:, :, None, None]
        pick = shifted[0]
        for c in range(1, 9):
            pick = jnp.where(code == c, shifted[c], pick)
        slots.append(pick)
    picked = jnp.stack(slots, axis=2)
    image = jnp.einsum("rakij,rakvj->ravi", jacobian, picked, preferred_element_type=jnp.float32)
    image = image.reshape(elements, NEW, BLK)

    moments = jnp.concatenate(
        [mm("epi,evi->pv", kept_flat, image), mm("evi,ewi->vw", image, image)], axis=0
    ).reshape(-1, BLK)
    split = kept_gram.shape[0]
    ahead = 2
    joint = all_sum(
        jnp.concatenate([kept_gram, moments], axis=0),
        [("rad", step) for step in radial[ahead:]] + around,
    )
    kept_gram, moments = joint[:split], joint[split:]
    for step in reversed(radial[:ahead]):
        other = exchange(jnp.concatenate([kept_gram, moments], axis=0), "rad", step)
        moments = moments + other[kept_gram.shape[0]:]
        kept_gram = join(kept_gram, other[: kept_gram.shape[0]], "rad", step)
    kept_gram = unpack_symmetric(kept_gram)
    moments = moments.reshape(KEEP + NEW, NEW)
    first, image_gram = moments[:KEEP], moments[KEEP:]

    second = first - mm("pq,qv->pv", kept_gram, first)
    coefficients = first + second

    cross = mm("pv,pw->vw", coefficients, first)
    expanded = (
        image_gram - cross - cross.T
        + mm("pv,pw->vw", coefficients, mm("pq,qw->pw", kept_gram, coefficients))
    ) / total_rows
    eye = jnp.eye(NEW, dtype=jnp.float32)
    kept_share = jnp.sum(expanded * eye, axis=1) * 16.0 >= jnp.sum(image_gram * eye, axis=1) / total_rows

    def factor_of(gram):
        lower = jnp.linalg.cholesky(gram, symmetrize_input=False)
        inverse = lax.linalg.triangular_solve(lower, eye, left_side=True, lower=True)
        return lower, inverse

    def expanded_path():
        lower, inverse = factor_of(expanded)
        fast = lax.Precision.HIGH
        basis = jnp.einsum(
            "evi,wv->ewi", image, inverse, precision=fast, preferred_element_type=jnp.float32
        ) - jnp.einsum(
            "epi,pw->ewi", kept_flat, mm("pv,wv->pw", coefficients, inverse),
            precision=fast, preferred_element_type=jnp.float32,
        )
        return basis, lower

    def direct_path():
        twice = image - mm("epi,pv->evi", kept_flat, coefficients)
        lower, inverse = factor_of(all_sum(mm("evi,ewi->vw", twice, twice), steps) / total_rows)
        return mm("evi,wv->ewi", twice, inverse), lower

    basis, lower = lax.cond(jnp.all(kept_share), expanded_path, direct_path)
    basis = basis.reshape(rows_r, rows_a, NEW, BLK)
    return (basis, coefficients, lower.T)


def solution(mesh):
    return jax.shard_map(
        on_device,
        mesh=mesh,
        in_specs=(
            P("rad", "azi", None, None, None),
            P("rad", "azi", None, None),
            P("rad", "azi", None, None),
            P("rad", "azi", None),
        ),
        out_specs=(P("rad", "azi", None, None), P(), P()),
        check_vma=False,
    )
```
